32 devices in a mesh: gx: 4 (over y, core), gy: 8 (over z, x).
Axes of the slice: x: 2, y: 2, z: 4, core: 2. Of those that a mesh axis runs over, the one named last changes fastest.
Arguments:
- mode_fields: float32 [64, 128, 512], P(None, 'gy', 'gx'), may hold values from -8 to 8
- mean_field: float32 [128, 512], P('gy', 'gx'), may hold values from 0.5 to 2
- coefficients: float32 [64, 16384], P(None, ('gx', 'gy')), may hold values from -40 to 40
Outputs:
- new_modes: float32 [64, 128, 512], P(None, 'gy', 'gx')
- new_mean: float32 [128, 512], P('gy', 'gx')
- new_coefficients: float32 [64, 16384], P(None, ('gx', 'gy'))
The draws below stay inside these ranges and needn't reach their ends.
All inputs are finite; a program needn't handle non-finite values.
Results may differ from the reference program's by a relative error of at most 0.0003.
Values sent between devices are 32-bit elements; how exact they have to be, the bound alone decides.
No kernel may reach another device: no remote copies, remote signals or barrier semaphores. Data moves between devices by JAX's collectives and lax.ppermute only.
A program may use at most 128 MiB of HBM per device.

```python
import jax
import jax.numpy as jnp
from jax import lax

M = 64
NS_ITERS = 6
NX = 512
NY = 128
R = 16384


def draw_mode_fields(key, part):
    subkeys = jax.random.split(key, 4)
    base_count = max(M // 4, 2)
    offsets = jax.random.uniform(subkeys[0], (M, 1, 1), jnp.float32, -0.7, 0.7)
    mixing = jax.random.normal(subkeys[1], (M, base_count), jnp.float32) / jnp.sqrt(jnp.float32(base_count))
    white_parts = jax.random.normal(subkeys[2], (base_count, NY, NX), jnp.float32)
    noise_part = jax.random.normal(subkeys[3], (M, NY, NX), jnp.float32)
    smooth = (white_parts + jnp.roll(white_parts, 1, axis=2) + jnp.roll(white_parts, 1, axis=1)) / jnp.sqrt(jnp.float32(3.0))
    base_fields = (smooth * smooth - 1.0) / jnp.sqrt(jnp.float32(2.0))
    mixture = jnp.dot(mixing, base_fields.reshape(base_count, NY * NX), precision=lax.Precision.HIGHEST).reshape(M, NY, NX)
    values = offsets + (0.85 * mixture + 0.6 * noise_part)
    return jnp.clip(values, -8.0, 8.0)


def draw_coefficients(key, part):
    subkeys = jax.random.split(key, 6)
    scales = jnp.exp(jax.random.uniform(subkeys[0], (M, 1), jnp.float32, -0.6931, 0.6931))
    skewness = jax.random.uniform(subkeys[1], (M, 1), jnp.float32, -0.3, 0.3)
    shared = jax.random.uniform(subkeys[2], (M, 1), jnp.float32, -0.3, 0.3)
    drifts = jax.random.uniform(subkeys[3], (M, 1), jnp.float32, -1.0, 1.0)
    private = jax.random.normal(subkeys[4], (M, R), jnp.float32)
    common = jax.random.normal(subkeys[5], (1, R), jnp.float32)
    position_ramp = 1.0 + 2.0 * jnp.arange(R, dtype=jnp.float32) / R
    values = scales * (private + skewness * (private * private - 1.0) + shared * (common * common - 1.0))
    values = values + drifts * scales * position_ramp[None, :]
    return jnp.clip(values, -40.0, 40.0)


def shard_levels(rng, shape, cuts, least, top_value):
    gain, own = 1.0, jax.random.fold_in(rng, 6)
    for axis_at, parts in cuts:
        steps = jnp.exp(jax.random.uniform(jax.random.fold_in(own, axis_at), (parts,), jnp.float32, least / len(cuts), top_value / len(cuts)))
        gain = gain * jnp.repeat(steps, shape[axis_at] // parts).reshape([-1 if axis == axis_at else 1 for axis in range(len(shape))])
    return gain


def setup_inputs(seed: int = 0) -> dict:
    key_of = jax.random.split(jax.random.key(seed), 4)
    return {
        "mode_fields": draw_mode_fields(jax.random.fold_in(key_of[3], 71), 0),
        "mean_field": jnp.clip(0.5 + 1.5 * jax.random.uniform(key_of[1], (NY, NX), jnp.float32) ** shard_levels(key_of[1], (NY, NX), ((0, 8), (1, 4)), -0.2, 0.2), 0.5, 2.0),
        "coefficients": draw_coefficients(jax.random.fold_in(key_of[3], 71), 0),
    }


TIME_STEP = 0.02
VISCOSITY = 0.25
PRECISE = lax.Precision.HIGHEST

def upwind(values):
    return 2.0 * values - jnp.roll(values, 1, axis=-1) - jnp.roll(values, 1, axis=-2)

def laplacian(values):
    beside_all = jnp.roll(values, 1, axis=-1) + jnp.roll(values, -1, axis=-1)
    beside_all = beside_all + jnp.roll(values, 1, axis=-2) + jnp.roll(values, -1, axis=-2)
    return beside_all - 4.0 * values

def inverse_root(covariance):
    identity = jnp.eye(covariance.shape[0], dtype=jnp.float32)
    scaling = jnp.sqrt(jnp.sum(covariance * covariance) + 1e-06)
    current = covariance / scaling
    inverse = identity
    for iteration in range(NS_ITERS):
        middle = 0.5 * (3.0 * identity - jnp.dot(inverse, current, precision=PRECISE))
        current = jnp.dot(current, middle, precision=PRECISE)
        inverse = jnp.dot(middle, inverse, precision=PRECISE)
    return inverse / jnp.sqrt(scaling)

def reference(mode_fields, mean_field, coefficients):
    cell_count = NX * NY
    samples = coefficients.shape[1]
    flattened = mode_fields.reshape(M, cell_count)
    gradient = upwind(mode_fields).reshape(M, cell_count)
    smoothed = laplacian(mode_fields).reshape(M, cell_count)
    mean_flat = mean_field.reshape(cell_count)
    mean_gradient = upwind(mean_field).reshape(cell_count)
    mean_smooth = laplacian(mean_field).reshape(cell_count)
    linear = -mean_flat * gradient - flattened * mean_gradient + VISCOSITY * smoothed
    coupling = jnp.dot(flattened, linear.T, precision=PRECISE) / cell_count

    def triad_row(position):
        product = flattened[position] * gradient
        return -jnp.dot(product, flattened.T, precision=PRECISE) / cell_count
    triads = lax.map(triad_row, jnp.arange(M, dtype=jnp.int32))
    sample_mean = lax.optimization_barrier(jnp.sum(coefficients, axis=1, keepdims=True)) / samples
    centered = coefficients - sample_mean
    covariance = jnp.dot(centered, centered.T, precision=PRECISE) / samples

    def third_row(position):
        return jnp.dot(centered[position] * centered, centered.T, precision=PRECISE) / samples
    third_moment = lax.map(third_row, jnp.arange(M, dtype=jnp.int32))

    def quad_step(total, position):
        weights = centered[position] * centered - covariance[position][:, None]
        return (total + jnp.dot(triads[position].T, weights, precision=PRECISE), None)
    quadratic, unused = lax.scan(quad_step, jnp.zeros((M, samples), jnp.float32), jnp.arange(M, dtype=jnp.int32))
    new_coefficients = centered + TIME_STEP * (jnp.dot(coupling, centered, precision=PRECISE) + quadratic)
    weighted = jnp.dot(covariance.T, flattened, precision=PRECISE)
    new_mean = mean_flat + TIME_STEP * (-mean_flat * mean_gradient + VISCOSITY * mean_smooth - lax.optimization_barrier(jnp.sum(weighted * gradient, axis=0)))

    def force_step(total, position):
        product = flattened[position] * gradient
        return (total + jnp.dot(third_moment[:, position, :], product, precision=PRECISE), None)
    moment_term, unused = lax.scan(force_step, jnp.zeros((M, cell_count), jnp.float32), jnp.arange(M, dtype=jnp.int32))
    forcing = jnp.dot(covariance, linear, precision=PRECISE) - moment_term
    projection = jnp.dot(forcing, flattened.T, precision=PRECISE) / cell_count
    residual = forcing - jnp.dot(projection, flattened, precision=PRECISE)
    half_power = inverse_root(covariance)
    weighting = jnp.dot(half_power, half_power, precision=PRECISE)
    stepped = flattened + TIME_STEP * jnp.dot(weighting, residual, precision=PRECISE)
    gram_matrix = jnp.dot(stepped, stepped.T, precision=PRECISE) / cell_count
    factor = jnp.linalg.cholesky(gram_matrix)
    new_modes = lax.linalg.triangular_solve(factor, stepped, left_side=True, lower=True)
    return (new_modes.reshape(M, NY, NX), new_mean.reshape(NY, NX), new_coefficients)
```

```python
import jax
import jax.numpy as jnp
import numpy as np
from jax import lax
from jax.sharding import PartitionSpec as P

NS_ITERS = 6


TIME_STEP = 0.02
VISCOSITY = 0.25
PRECISE = lax.Precision.HIGHEST


AXES = ("gx", "gy")


def device_count():
    return lax.axis_size("gx") * lax.axis_size("gy")


def linear_index():
    return lax.axis_index("gx") * lax.axis_size("gy") + lax.axis_index("gy")


def exchange_bits():
    count = device_count()
    bits = [1 << b for b in range(count.bit_length() - 1)]
    first = lax.axis_size("gy")
    return [first] + [bit for bit in bits if bit != first]


def swap(values, bit):
    count = device_count()
    return lax.ppermute(values, AXES, [(i, i ^ bit) for i in range(count)])


def doubling_sum(values):
    count = device_count()
    if count & (count - 1):
        return lax.psum(values, AXES)
    for bit in exchange_bits():
        values = values + swap(values, bit)
    return values


def halving_sum(parts):
    count = device_count()
    if count & (count - 1):
        return lax.psum(parts, AXES)
    shapes = [part.shape for part in parts]
    flat = jnp.concatenate([part.reshape(-1) for part in parts])
    total = flat.shape[0]
    unit = count * 128
    padded = -(-total // unit) * unit
    flat = jnp.pad(flat, (0, padded - total)).reshape(padded // 128, 128)
    me = linear_index()
    bits = exchange_bits()
    for bit in bits:
        half = flat.shape[0] // 2
        upper = (me // bit) % 2
        keep = lax.dynamic_slice_in_dim(flat, upper * half, half)
        send = lax.dynamic_slice_in_dim(flat, (1 - upper) * half, half)
        flat = keep + swap(send, bit)
    for bit in reversed(bits):
        upper = (me // bit) % 2
        other = swap(flat, bit)
        both = jnp.zeros((2 * flat.shape[0], 128), flat.dtype)
        both = lax.dynamic_update_slice_in_dim(both, flat, upper * flat.shape[0], 0)
        flat = lax.dynamic_update_slice_in_dim(both, other, (1 - upper) * flat.shape[0], 0)
    flat = flat.reshape(-1)[:total]
    out, start = [], 0
    for shape in shapes:
        size = int(np.prod(shape))
        out.append(flat[start:start + size].reshape(shape))
        start += size
    return out


def padded_2(array, sides, width):
    for axis, dim in sides:
        size, length = (lax.axis_size(axis), array.shape[dim])
        up = [(i, (i + 1) % size) for i in range(size)]
        down = [(j, i) for i, j in up]
        last = lax.slice_in_dim(array, length - width, length, axis=dim)
        first = lax.slice_in_dim(array, 0, width, axis=dim)
        before = lax.ppermute(last, axis, up)
        after = lax.ppermute(first, axis, down)
        array = jnp.concatenate([before, array, after], axis=dim)
    return array


def matmul(left, right):
    return jnp.dot(left, right, precision=PRECISE)


def pair_index(extent):
    flat_pairs = np.arange(extent * extent)
    leading = flat_pairs // extent
    trailing = flat_pairs % extent
    return (leading, trailing)


def pair_rows(values):
    extent = values.shape[0]
    return (values[:, None, :] * values[None, :, :]).reshape(extent * extent, values.shape[1])


def inverse_root(covariance):
    identity = jnp.eye(covariance.shape[0], dtype=jnp.float32)
    scaling = jnp.sqrt(jnp.sum(covariance * covariance) + 1e-06)
    current = covariance / scaling
    inverse = identity
    for iteration in range(NS_ITERS):
        middle = 0.5 * (3.0 * identity - matmul(inverse, current))
        current = matmul(current, middle)
        inverse = matmul(middle, inverse)
    return inverse / jnp.sqrt(scaling)


def per_device(mode_fields, mean_field, coefficients):
    extent = mode_fields.shape[0]
    devices = lax.axis_size("gx") * lax.axis_size("gy")
    local_cells = mode_fields.shape[1] * mode_fields.shape[2]
    cell_count = local_cells * devices
    samples = coefficients.shape[1] * devices
    stacked = jnp.concatenate([mean_field[None], mode_fields], axis=0)
    padded = padded_2(stacked, (("gx", 2), ("gy", 1)), 1)
    middle = padded[:, 1:-1, 1:-1]
    western = padded[:, 1:-1, :-2]
    eastern = padded[:, 1:-1, 2:]
    southern = padded[:, :-2, 1:-1]
    northern = padded[:, 2:, 1:-1]
    upwinded = (2.0 * middle - western - southern).reshape(extent + 1, local_cells)
    smoothed = (western + eastern + southern + northern - 4.0 * middle).reshape(
        extent + 1, local_cells
    )
    mean_flat = mean_field.reshape(local_cells)
    mean_gradient = upwinded[0]
    mean_smooth = smoothed[0]
    gradient = upwinded[1:]
    flattened = mode_fields.reshape(extent, local_cells)
    linear = -mean_flat * gradient - flattened * mean_gradient + VISCOSITY * smoothed[1:]
    coupling_part = matmul(flattened, linear.T)
    products = (flattened[:, None, :] * gradient[None, :, :]).reshape(extent * extent, local_cells)
    triad_full = -matmul(products, flattened.T)
    totals = doubling_sum(jnp.sum(coefficients, axis=1))
    sample_mean = totals / samples
    centered = coefficients - sample_mean[:, None]
    pairs = pair_rows(centered)
    triads, coupling, covariance, third_moment = halving_sum(
        [triad_full, coupling_part, matmul(centered, centered.T), matmul(pairs, centered.T)]
    )
    covariance = covariance / samples
    third_moment = third_moment / samples
    triads = triads / cell_count
    coupling = coupling / cell_count
    weights = pairs - covariance.reshape(extent * extent)[:, None]
    quadratic = lax.dot_general(triads, weights, (((0,), (0,)), ((), ())), precision=PRECISE)
    new_coefficients = centered + TIME_STEP * (matmul(coupling, centered) + quadratic)
    weighted = matmul(covariance.T, flattened)
    new_mean = mean_flat + TIME_STEP * (
        -mean_flat * mean_gradient + VISCOSITY * mean_smooth - jnp.sum(weighted * gradient, axis=0)
    )
    moment_flat = third_moment.reshape(extent, extent * extent)
    moment_term = matmul(moment_flat, products)
    forcing = matmul(covariance, linear) - moment_term
    half_power = inverse_root(covariance)
    weighting = matmul(half_power, half_power)
    projection = matmul(covariance, coupling.T) + matmul(moment_flat, triads)
    residual = forcing - matmul(projection, flattened)
    stepped = flattened + TIME_STEP * matmul(weighting, residual)
    gram_matrix = doubling_sum(matmul(stepped, stepped.T)) / cell_count
    factor = jnp.linalg.cholesky(gram_matrix)
    new_modes = lax.linalg.triangular_solve(factor, stepped, left_side=True, lower=True)
    return (
        new_modes.reshape(mode_fields.shape),
        new_mean.reshape(mean_field.shape),
        new_coefficients,
    )


def solution(mesh):
    placed = (P(None, "gy", "gx"), P("gy", "gx"), P(None, ("gx", "gy")))
    return jax.shard_map(
        per_device,
        mesh=mesh,
        in_specs=placed,
        out_specs=(P(None, "gy", "gx"), P("gy", "gx"), P(None, ("gx", "gy"))),
        check_vma=False,
    )
```

```python
import jax
import jax.numpy as jnp
import numpy as np
from jax import lax
from jax.sharding import PartitionSpec as P

NS_ITERS = 6


TIME_STEP = 0.02
VISCOSITY = 0.25
PRECISE = lax.Precision.HIGHEST


AXES = ("gx", "gy")


def device_count():
    return lax.axis_size("gx") * lax.axis_size("gy")


def linear_index():
    return lax.axis_index("gx") * lax.axis_size("gy") + lax.axis_index("gy")


def exchange_bits():
    count = device_count()
    bits = [1 << b for b in range(count.bit_length() - 1)]
    first = lax.axis_size("gy")
    return [first] + [bit for bit in bits if bit != first]


def swap(values, bit):
    count = device_count()
    return lax.ppermute(values, AXES, [(i, i ^ bit) for i in range(count)])


def doubling_sum(values):
    count = device_count()
    if count & (count - 1):
        return lax.psum(values, AXES)
    for bit in exchange_bits():
        values = values + swap(values, bit)
    return values


def halving_sum(parts):
    count = device_count()
    if count & (count - 1):
        return lax.psum(parts, AXES)
    shapes = [part.shape for part in parts]
    flat = jnp.concatenate([part.reshape(-1) for part in parts])
    total = flat.shape[0]
    unit = count * 128
    padded = -(-total // unit) * unit
    flat = jnp.pad(flat, (0, padded - total)).reshape(padded // 128, 128)
    me = linear_index()
    bits = exchange_bits()
    for bit in bits:
        half = flat.shape[0] // 2
        upper = (me // bit) % 2
        keep = lax.dynamic_slice_in_dim(flat, upper * half, half)
        send = lax.dynamic_slice_in_dim(flat, (1 - upper) * half, half)
        flat = keep + swap(send, bit)
    for bit in reversed(bits):
        upper = (me // bit) % 2
        other = swap(flat, bit)
        both = jnp.zeros((2 * flat.shape[0], 128), flat.dtype)
        both = lax.dynamic_update_slice_in_dim(both, flat, upper * flat.shape[0], 0)
        flat = lax.dynamic_update_slice_in_dim(both, other, (1 - upper) * flat.shape[0], 0)
    flat = flat.reshape(-1)[:total]
    out, start = [], 0
    for shape in shapes:
        size = int(np.prod(shape))
        out.append(flat[start:start + size].reshape(shape))
        start += size
    return out


def padded_2(array, sides, width):
    for axis, dim in sides:
        size, length = (lax.axis_size(axis), array.shape[dim])
        up = [(i, (i + 1) % size) for i in range(size)]
        down = [(j, i) for i, j in up]
        last = lax.slice_in_dim(array, length - width, length, axis=dim)
        first = lax.slice_in_dim(array, 0, width, axis=dim)
        before = lax.ppermute(last, axis, up)
        after = lax.ppermute(first, axis, down)
        array = jnp.concatenate([before, array, after], axis=dim)
    return array


def matmul(left, right):
    return jnp.dot(left, right, precision=PRECISE)


def symmetric_rows(left, right):
    extent = left.shape[0]
    half = extent // 2
    rows = [left * right]
    for offset in range(1, (extent + 1) // 2):
        rows.append(left * jnp.roll(right, -offset, axis=0) + jnp.roll(left, -offset, axis=0) * right)
    if extent % 2 == 0:
        rows.append(left[:half] * right[half:] + left[half:] * right[:half])
    return jnp.concatenate(rows, axis=0)


def symmetric_squares(values):
    extent = values.shape[0]
    half = extent // 2
    rows = [values * values]
    for offset in range(1, (extent + 1) // 2):
        rows.append(values * jnp.roll(values, -offset, axis=0))
    if extent % 2 == 0:
        rows.append(values[:half] * values[half:])
    return jnp.concatenate(rows, axis=0)


def contract_rows(left, right):
    return lax.dot_general(left, right, (((0,), (0,)), ((), ())), precision=PRECISE)


def inverse_root(covariance):
    identity = jnp.eye(covariance.shape[0], dtype=jnp.float32)
    scaling = jnp.sqrt(jnp.sum(covariance * covariance) + 1e-06)
    current = covariance / scaling
    inverse = identity
    for iteration in range(NS_ITERS):
        middle = 0.5 * (3.0 * identity - matmul(inverse, current))
        current = matmul(current, middle)
        inverse = matmul(middle, inverse)
    return inverse / jnp.sqrt(scaling)


def per_device(mode_fields, mean_field, coefficients):
    extent = mode_fields.shape[0]
    devices = lax.axis_size("gx") * lax.axis_size("gy")
    local_cells = mode_fields.shape[1] * mode_fields.shape[2]
    cell_count = local_cells * devices
    samples = coefficients.shape[1] * devices
    stacked = jnp.concatenate([mean_field[None], mode_fields], axis=0)
    padded = padded_2(stacked, (("gx", 2), ("gy", 1)), 1)
    middle = padded[:, 1:-1, 1:-1]
    western = padded[:, 1:-1, :-2]
    eastern = padded[:, 1:-1, 2:]
    southern = padded[:, :-2, 1:-1]
    northern = padded[:, 2:, 1:-1]
    upwinded = (2.0 * middle - western - southern).reshape(extent + 1, local_cells)
    smoothed = (western + eastern + southern + northern - 4.0 * middle).reshape(
        extent + 1, local_cells
    )
    mean_flat = mean_field.reshape(local_cells)
    mean_gradient = upwinded[0]
    mean_smooth = smoothed[0]
    gradient = upwinded[1:]
    flattened = mode_fields.reshape(extent, local_cells)
    linear = -mean_flat * gradient - flattened * mean_gradient + VISCOSITY * smoothed[1:]
    coupling_part = matmul(flattened, linear.T)
    products = symmetric_rows(flattened, gradient)
    triad_part = -matmul(products, flattened.T)
    totals = doubling_sum(jnp.sum(coefficients, axis=1))
    sample_mean = totals / samples
    centered = coefficients - sample_mean[:, None]
    pairs = symmetric_squares(centered)
    triads, coupling, covariance, pair_cov, third_moment = halving_sum(
        [triad_part, coupling_part, matmul(centered, centered.T), jnp.sum(pairs, axis=1),
         matmul(pairs, centered.T)]
    )
    covariance = covariance / samples
    pair_cov = pair_cov / samples
    third_moment = third_moment / samples
    triads = triads / cell_count
    coupling = coupling / cell_count
    quadratic = contract_rows(triads, pairs - pair_cov[:, None])
    new_coefficients = centered + TIME_STEP * (matmul(coupling, centered) + quadratic)
    weighted = matmul(covariance.T, flattened)
    new_mean = mean_flat + TIME_STEP * (
        -mean_flat * mean_gradient + VISCOSITY * mean_smooth - jnp.sum(weighted * gradient, axis=0)
    )
    moment_term = contract_rows(third_moment, products)
    forcing = matmul(covariance, linear) - moment_term
    half_power = inverse_root(covariance)
    weighting = matmul(half_power, half_power)
    projection = matmul(covariance, coupling.T) + contract_rows(third_moment, triads)
    residual = forcing - matmul(projection, flattened)
    stepped = flattened + TIME_STEP * matmul(weighting, residual)
    gram_matrix = doubling_sum(matmul(stepped, stepped.T)) / cell_count
    factor = jnp.linalg.cholesky(gram_matrix)
    new_modes = lax.linalg.triangular_solve(factor, stepped, left_side=True, lower=True)
    return (
        new_modes.reshape(mode_fields.shape),
        new_mean.reshape(mean_field.shape),
        new_coefficients,
    )


def solution(mesh):
    placed = (P(None, "gy", "gx"), P("gy", "gx"), P(None, ("gx", "gy")))
    return jax.shard_map(
        per_device,
        mesh=mesh,
        in_specs=placed,
        out_specs=(P(None, "gy", "gx"), P("gy", "gx"), P(None, ("gx", "gy"))),
        check_vma=False,
    )
```

```python
import jax
import jax.numpy as jnp
import numpy as np
from jax import lax
from jax.sharding import PartitionSpec as P

NS_ITERS = 6


TIME_STEP = 0.02
VISCOSITY = 0.25
PRECISE = lax.Precision.HIGHEST


AXES = ("gx", "gy")


def device_count():
    return lax.axis_size("gx") * lax.axis_size("gy")


def linear_index():
    return lax.axis_index("gx") * lax.axis_size("gy") + lax.axis_index("gy")


def exchange_bits():
    count = device_count()
    bits = [1 << b for b in range(count.bit_length() - 1)]
    first = lax.axis_size("gy")
    return [first] + [bit for bit in bits if bit != first]


def swap(values, bit):
    count = device_count()
    return lax.ppermute(values, AXES, [(i, i ^ bit) for i in range(count)])


def doubling_sum(values):
    count = device_count()
    if count & (count - 1):
        return lax.psum(values, AXES)
    for bit in exchange_bits():
        values = values + swap(values, bit)
    return values


def halving_sum(parts):
    count = device_count()
    if count & (count - 1):
        return lax.psum(parts, AXES)
    shapes = [part.shape for part in parts]
    flat = jnp.concatenate([part.reshape(-1) for part in parts])
    total = flat.shape[0]
    unit = count * 128
    padded = -(-total // unit) * unit
    flat = jnp.pad(flat, (0, padded - total)).reshape(padded // 128, 128)
    me = linear_index()
    bits = exchange_bits()
    for bit in bits:
        half = flat.shape[0] // 2
        upper = (me // bit) % 2
        keep = lax.dynamic_slice_in_dim(flat, upper * half, half)
        send = lax.dynamic_slice_in_dim(flat, (1 - upper) * half, half)
        flat = keep + swap(send, bit)
    for bit in reversed(bits):
        upper = (me // bit) % 2
        other = swap(flat, bit)
        both = jnp.zeros((2 * flat.shape[0], 128), flat.dtype)
        both = lax.dynamic_update_slice_in_dim(both, flat, upper * flat.shape[0], 0)
        flat = lax.dynamic_update_slice_in_dim(both, other, (1 - upper) * flat.shape[0], 0)
    flat = flat.reshape(-1)[:total]
    out, start = [], 0
    for shape in shapes:
        size = int(np.prod(shape))
        out.append(flat[start:start + size].reshape(shape))
        start += size
    return out


def padded_2(array, sides, width):
    for axis, dim in sides:
        size, length = (lax.axis_size(axis), array.shape[dim])
        up = [(i, (i + 1) % size) for i in range(size)]
        down = [(j, i) for i, j in up]
        last = lax.slice_in_dim(array, length - width, length, axis=dim)
        first = lax.slice_in_dim(array, 0, width, axis=dim)
        before = lax.ppermute(last, axis, up)
        after = lax.ppermute(first, axis, down)
        array = jnp.concatenate([before, array, after], axis=dim)
    return array


def matmul(left, right):
    return jnp.dot(left, right, precision=PRECISE)


def pair_blocks(extent):
    return extent // 2 + 1


def repeated(values):
    blocks = pair_blocks(values.shape[0])
    spread = jnp.broadcast_to(values[None], (blocks,) + values.shape)
    return spread.reshape((blocks * values.shape[0],) + values.shape[1:])


def shifted(values):
    extent = values.shape[0]
    blocks = pair_blocks(extent)
    copies = -(-(blocks * (extent + 1)) // extent)
    spread = jnp.broadcast_to(values[None], (copies,) + values.shape)
    spread = spread.reshape((copies * extent,) + values.shape[1:])[: blocks * (extent + 1)]
    window = spread.reshape((blocks, extent + 1) + values.shape[1:])[:, :extent]
    return window.reshape((blocks * extent,) + values.shape[1:])


def pair_weights(extent):
    weights = np.ones((pair_blocks(extent), extent), np.float32)
    weights[0] = 0.5
    if extent % 2 == 0:
        weights[-1] = 0.5
    return weights.reshape(-1)


def symmetric_rows(left, right):
    weights = pair_weights(left.shape[0]).reshape((-1,) + (1,) * (left.ndim - 1))
    return (repeated(left) * shifted(right) + shifted(left) * repeated(right)) * weights


def symmetric_squares(values):
    return repeated(values) * shifted(values)


def contract_rows(left, right):
    return lax.dot_general(left, right, (((0,), (0,)), ((), ())), precision=PRECISE)


def inverse_root(covariance):
    identity = jnp.eye(covariance.shape[0], dtype=jnp.float32)
    scaling = jnp.sqrt(jnp.sum(covariance * covariance) + 1e-06)
    current = covariance / scaling
    inverse = identity
    for iteration in range(NS_ITERS):
        middle = 0.5 * (3.0 * identity - matmul(inverse, current))
        current = matmul(current, middle)
        inverse = matmul(middle, inverse)
    return inverse / jnp.sqrt(scaling)


def per_device(mode_fields, mean_field, coefficients):
    extent = mode_fields.shape[0]
    devices = lax.axis_size("gx") * lax.axis_size("gy")
    local_cells = mode_fields.shape[1] * mode_fields.shape[2]
    cell_count = local_cells * devices
    samples = coefficients.shape[1] * devices
    stacked = jnp.concatenate([mean_field[None], mode_fields], axis=0)
    padded = padded_2(stacked, (("gx", 2), ("gy", 1)), 1)
    middle = padded[:, 1:-1, 1:-1]
    western = padded[:, 1:-1, :-2]
    eastern = padded[:, 1:-1, 2:]
    southern = padded[:, :-2, 1:-1]
    northern = padded[:, 2:, 1:-1]
    upwinded = (2.0 * middle - western - southern).reshape(extent + 1, local_cells)
    smoothed = (western + eastern + southern + northern - 4.0 * middle).reshape(
        extent + 1, local_cells
    )
    mean_flat = mean_field.reshape(local_cells)
    mean_gradient = upwinded[0]
    mean_smooth = smoothed[0]
    gradient = upwinded[1:]
    flattened = mode_fields.reshape(extent, local_cells)
    linear = -mean_flat * gradient - flattened * mean_gradient + VISCOSITY * smoothed[1:]
    coupling_part = matmul(flattened, linear.T)
    products = symmetric_rows(mode_fields, upwinded[1:].reshape(mode_fields.shape))
    triad_part = -lax.dot_general(
        products, mode_fields, (((1, 2), (1, 2)), ((), ())), precision=PRECISE
    )
    totals = doubling_sum(jnp.sum(coefficients, axis=1))
    sample_mean = totals / samples
    centered = coefficients - sample_mean[:, None]
    pairs = symmetric_squares(centered)
    triads, coupling, covariance, pair_cov, third_moment = halving_sum(
        [triad_part, coupling_part, matmul(centered, centered.T), jnp.sum(pairs, axis=1),
         matmul(pairs, centered.T)]
    )
    covariance = covariance / samples
    pair_cov = pair_cov / samples
    third_moment = third_moment / samples
    triads = triads / cell_count
    coupling = coupling / cell_count
    quadratic = contract_rows(triads, pairs - pair_cov[:, None])
    new_coefficients = centered + TIME_STEP * (matmul(coupling, centered) + quadratic)
    weighted = matmul(covariance.T, flattened)
    new_mean = mean_flat + TIME_STEP * (
        -mean_flat * mean_gradient + VISCOSITY * mean_smooth - jnp.sum(weighted * gradient, axis=0)
    )
    moment_term = contract_rows(third_moment, products).reshape(extent, local_cells)
    forcing = matmul(covariance, linear) - moment_term
    half_power = inverse_root(covariance)
    weighting = matmul(half_power, half_power)
    projection = matmul(covariance, coupling.T) + contract_rows(third_moment, triads)
    residual = forcing - matmul(projection, flattened)
    stepped = flattened + TIME_STEP * matmul(weighting, residual)
    gram_matrix = doubling_sum(matmul(stepped, stepped.T)) / cell_count
    factor = jnp.linalg.cholesky(gram_matrix)
    new_modes = lax.linalg.triangular_solve(factor, stepped, left_side=True, lower=True)
    return (
        new_modes.reshape(mode_fields.shape),
        new_mean.reshape(mean_field.shape),
        new_coefficients,
    )


def solution(mesh):
    placed = (P(None, "gy", "gx"), P("gy", "gx"), P(None, ("gx", "gy")))
    return jax.shard_map(
        per_device,
        mesh=mesh,
        in_specs=placed,
        out_specs=(P(None, "gy", "gx"), P("gy", "gx"), P(None, ("gx", "gy"))),
        check_vma=False,
    )
```

```python
import jax
import jax.numpy as jnp
import numpy as np
from jax import lax
from jax.sharding import PartitionSpec as P

NS_ITERS = 6


TIME_STEP = 0.02
VISCOSITY = 0.25
PRECISE = lax.Precision.HIGHEST
FAST = lax.Precision.HIGH


AXES = ("gx", "gy")


def device_count():
    return lax.axis_size("gx") * lax.axis_size("gy")


def linear_index():
    return lax.axis_index("gx") * lax.axis_size("gy") + lax.axis_index("gy")


def exchange_bits():
    count = device_count()
    bits = [1 << b for b in range(count.bit_length() - 1)]
    first = lax.axis_size("gy")
    return [first] + [bit for bit in bits if bit != first]


def swap(values, bit):
    count = device_count()
    return lax.ppermute(values, AXES, [(i, i ^ bit) for i in range(count)])


def doubling_sum(values):
    count = device_count()
    if count & (count - 1):
        return lax.psum(values, AXES)
    for bit in exchange_bits():
        values = values + swap(values, bit)
    return values


def halving_sum(parts):
    count = device_count()
    if count & (count - 1):
        return lax.psum(parts, AXES)
    shapes = [part.shape for part in parts]
    flat = jnp.concatenate([part.reshape(-1) for part in parts])
    total = flat.shape[0]
    unit = count * 128
    padded = -(-total // unit) * unit
    flat = jnp.pad(flat, (0, padded - total)).reshape(padded // 128, 128)
    me = linear_index()
    bits = exchange_bits()
    for bit in bits:
        half = flat.shape[0] // 2
        upper = (me // bit) % 2
        keep = lax.dynamic_slice_in_dim(flat, upper * half, half)
        send = lax.dynamic_slice_in_dim(flat, (1 - upper) * half, half)
        flat = keep + swap(send, bit)
    for bit in reversed(bits):
        upper = (me // bit) % 2
        other = swap(flat, bit)
        both = jnp.zeros((2 * flat.shape[0], 128), flat.dtype)
        both = lax.dynamic_update_slice_in_dim(both, flat, upper * flat.shape[0], 0)
        flat = lax.dynamic_update_slice_in_dim(both, other, (1 - upper) * flat.shape[0], 0)
    flat = flat.reshape(-1)[:total]
    out, start = [], 0
    for shape in shapes:
        size = int(np.prod(shape))
        out.append(flat[start:start + size].reshape(shape))
        start += size
    return out


def padded_2(array, sides, width):
    for axis, dim in sides:
        size, length = (lax.axis_size(axis), array.shape[dim])
        up = [(i, (i + 1) % size) for i in range(size)]
        down = [(j, i) for i, j in up]
        last = lax.slice_in_dim(array, length - width, length, axis=dim)
        first = lax.slice_in_dim(array, 0, width, axis=dim)
        before = lax.ppermute(last, axis, up)
        after = lax.ppermute(first, axis, down)
        array = jnp.concatenate([before, array, after], axis=dim)
    return array


def matmul(left, right):
    return jnp.dot(left, right, precision=PRECISE)


def fast_matmul(left, right):
    return jnp.dot(left, right, precision=FAST)


def pair_index(extent):
    flat_pairs = np.arange(extent * extent)
    leading = flat_pairs // extent
    trailing = flat_pairs % extent
    return (leading, trailing)


def pair_rows(values):
    extent = values.shape[0]
    return (values[:, None, :] * values[None, :, :]).reshape(extent * extent, values.shape[1])


def inverse_root(covariance):
    identity = jnp.eye(covariance.shape[0], dtype=jnp.float32)
    scaling = jnp.sqrt(jnp.sum(covariance * covariance) + 1e-06)
    current = covariance / scaling
    inverse = identity
    for iteration in range(NS_ITERS):
        middle = 0.5 * (3.0 * identity - matmul(inverse, current))
        current = matmul(current, middle)
        inverse = matmul(middle, inverse)
    return inverse / jnp.sqrt(scaling)


def per_device(mode_fields, mean_field, coefficients):
    extent = mode_fields.shape[0]
    devices = lax.axis_size("gx") * lax.axis_size("gy")
    local_cells = mode_fields.shape[1] * mode_fields.shape[2]
    cell_count = local_cells * devices
    samples = coefficients.shape[1] * devices
    stacked = jnp.concatenate([mean_field[None], mode_fields], axis=0)
    padded = padded_2(stacked, (("gx", 2), ("gy", 1)), 1)
    middle = padded[:, 1:-1, 1:-1]
    western = padded[:, 1:-1, :-2]
    eastern = padded[:, 1:-1, 2:]
    southern = padded[:, :-2, 1:-1]
    northern = padded[:, 2:, 1:-1]
    upwinded = (2.0 * middle - western - southern).reshape(extent + 1, local_cells)
    smoothed = (western + eastern + southern + northern - 4.0 * middle).reshape(
        extent + 1, local_cells
    )
    mean_flat = mean_field.reshape(local_cells)
    mean_gradient = upwinded[0]
    mean_smooth = smoothed[0]
    gradient = upwinded[1:]
    flattened = mode_fields.reshape(extent, local_cells)
    linear = -mean_flat * gradient - flattened * mean_gradient + VISCOSITY * smoothed[1:]
    coupling_part = matmul(flattened, linear.T)
    products = (flattened[:, None, :] * gradient[None, :, :]).reshape(extent * extent, local_cells)
    triad_full = -fast_matmul(products, flattened.T)
    totals = doubling_sum(jnp.sum(coefficients, axis=1))
    sample_mean = totals / samples
    centered = coefficients - sample_mean[:, None]
    pairs = pair_rows(centered)
    triads, coupling, covariance, third_moment = halving_sum(
        [triad_full, coupling_part, matmul(centered, centered.T), fast_matmul(pairs, centered.T)]
    )
    covariance = covariance / samples
    third_moment = third_moment / samples
    triads = triads / cell_count
    coupling = coupling / cell_count
    weights = pairs - covariance.reshape(extent * extent)[:, None]
    quadratic = lax.dot_general(triads, weights, (((0,), (0,)), ((), ())), precision=FAST)
    new_coefficients = centered + TIME_STEP * (matmul(coupling, centered) + quadratic)
    weighted = matmul(covariance.T, flattened)
    new_mean = mean_flat + TIME_STEP * (
        -mean_flat * mean_gradient + VISCOSITY * mean_smooth - jnp.sum(weighted * gradient, axis=0)
    )
    moment_flat = third_moment.reshape(extent, extent * extent)
    moment_term = fast_matmul(moment_flat, products)
    forcing = matmul(covariance, linear) - moment_term
    half_power = inverse_root(covariance)
    weighting = matmul(half_power, half_power)
    projection = matmul(covariance, coupling.T) + matmul(moment_flat, triads)
    residual = forcing - matmul(projection, flattened)
    stepped = flattened + TIME_STEP * matmul(weighting, residual)
    gram_matrix = doubling_sum(matmul(stepped, stepped.T)) / cell_count
    factor = jnp.linalg.cholesky(gram_matrix)
    new_modes = lax.linalg.triangular_solve(factor, stepped, left_side=True, lower=True)
    return (
        new_modes.reshape(mode_fields.shape),
        new_mean.reshape(mean_field.shape),
        new_coefficients,
    )


def solution(mesh):
    placed = (P(None, "gy", "gx"), P("gy", "gx"), P(None, ("gx", "gy")))
    return jax.shard_map(
        per_device,
        mesh=mesh,
        in_specs=placed,
        out_specs=(P(None, "gy", "gx"), P("gy", "gx"), P(None, ("gx", "gy"))),
        check_vma=False,
    )
```

```python
import jax
import jax.numpy as jnp
import numpy as np
from jax import lax
from jax.sharding import PartitionSpec as P

NS_ITERS = 6


TIME_STEP = 0.02
VISCOSITY = 0.25
PRECISE = lax.Precision.HIGHEST
FAST = lax.Precision.HIGH


AXES = ("gx", "gy")


def device_count():
    return lax.axis_size("gx") * lax.axis_size("gy")


def linear_index():
    return lax.axis_index("gx") * lax.axis_size("gy") + lax.axis_index("gy")


def exchange_bits():
    count = device_count()
    bits = [1 << b for b in range(count.bit_length() - 1)]
    first = lax.axis_size("gy")
    return [first] + [bit for bit in bits if bit != first]


def swap(values, bit):
    count = device_count()
    return lax.ppermute(values, AXES, [(i, i ^ bit) for i in range(count)])


def doubling_sum(values):
    count = device_count()
    if count & (count - 1):
        return lax.psum(values, AXES)
    for bit in exchange_bits():
        values = values + swap(values, bit)
    return values


def halving_sum(parts):
    count = device_count()
    if count & (count - 1):
        return lax.psum(parts, AXES)
    shapes = [part.shape for part in parts]
    flat = jnp.concatenate([part.reshape(-1) for part in parts])
    total = flat.shape[0]
    unit = count * 128
    padded = -(-total // unit) * unit
    flat = jnp.pad(flat, (0, padded - total)).reshape(padded // 128, 128)
    me = linear_index()
    bits = exchange_bits()
    for bit in bits:
        half = flat.shape[0] // 2
        upper = (me // bit) % 2
        keep = lax.dynamic_slice_in_dim(flat, upper * half, half)
        send = lax.dynamic_slice_in_dim(flat, (1 - upper) * half, half)
        flat = keep + swap(send, bit)
    for bit in reversed(bits):
        upper = (me // bit) % 2
        other = swap(flat, bit)
        both = jnp.zeros((2 * flat.shape[0], 128), flat.dtype)
        both = lax.dynamic_update_slice_in_dim(both, flat, upper * flat.shape[0], 0)
        flat = lax.dynamic_update_slice_in_dim(both, other, (1 - upper) * flat.shape[0], 0)
    flat = flat.reshape(-1)[:total]
    out, start = [], 0
    for shape in shapes:
        size = int(np.prod(shape))
        out.append(flat[start:start + size].reshape(shape))
        start += size
    return out


def padded_2(array, sides, width):
    for axis, dim in sides:
        size, length = (lax.axis_size(axis), array.shape[dim])
        up = [(i, (i + 1) % size) for i in range(size)]
        down = [(j, i) for i, j in up]
        last = lax.slice_in_dim(array, length - width, length, axis=dim)
        first = lax.slice_in_dim(array, 0, width, axis=dim)
        before = lax.ppermute(last, axis, up)
        after = lax.ppermute(first, axis, down)
        array = jnp.concatenate([before, array, after], axis=dim)
    return array


def matmul(left, right):
    return jnp.dot(left, right, precision=PRECISE)


def fast_matmul(left, right):
    return jnp.dot(left, right, precision=FAST)


def pair_index(extent):
    flat_pairs = np.arange(extent * extent)
    leading = flat_pairs // extent
    trailing = flat_pairs % extent
    return (leading, trailing)


def pair_rows(values):
    extent = values.shape[0]
    return (values[:, None, :] * values[None, :, :]).reshape(extent * extent, values.shape[1])


def inverse_root(covariance):
    identity = jnp.eye(covariance.shape[0], dtype=jnp.float32)
    scaling = jnp.sqrt(jnp.sum(covariance * covariance) + 1e-06)
    current = covariance / scaling
    inverse = identity
    for iteration in range(NS_ITERS):
        middle = 0.5 * (3.0 * identity - matmul(inverse, current))
        current = matmul(current, middle)
        inverse = matmul(middle, inverse)
    return inverse / jnp.sqrt(scaling)


def per_device(mode_fields, mean_field, coefficients):
    extent = mode_fields.shape[0]
    devices = lax.axis_size("gx") * lax.axis_size("gy")
    local_cells = mode_fields.shape[1] * mode_fields.shape[2]
    cell_count = local_cells * devices
    samples = coefficients.shape[1] * devices
    stacked = jnp.concatenate([mean_field[None], mode_fields], axis=0)
    padded = padded_2(stacked, (("gx", 2), ("gy", 1)), 1)
    middle = padded[:, 1:-1, 1:-1]
    western = padded[:, 1:-1, :-2]
    eastern = padded[:, 1:-1, 2:]
    southern = padded[:, :-2, 1:-1]
    northern = padded[:, 2:, 1:-1]
    upwinded = (2.0 * middle - western - southern).reshape(extent + 1, local_cells)
    smoothed = (western + eastern + southern + northern - 4.0 * middle).reshape(
        extent + 1, local_cells
    )
    mean_flat = mean_field.reshape(local_cells)
    mean_gradient = upwinded[0]
    mean_smooth = smoothed[0]
    gradient = upwinded[1:]
    flattened = mode_fields.reshape(extent, local_cells)
    linear = -mean_flat * gradient - flattened * mean_gradient + VISCOSITY * smoothed[1:]
    coupling_part = matmul(flattened, linear.T)
    products = (flattened[:, None, :] * gradient[None, :, :]).reshape(extent * extent, local_cells)
    triad_full = -fast_matmul(products, flattened.T)
    totals = doubling_sum(jnp.sum(coefficients, axis=1))
    sample_mean = totals / samples
    centered = coefficients - sample_mean[:, None]
    pairs = pair_rows(centered)
    covariance, third_moment = halving_sum(
        [matmul(centered, centered.T), fast_matmul(pairs, centered.T)]
    )
    triads, coupling = halving_sum([triad_full, coupling_part])
    covariance = covariance / samples
    third_moment = third_moment / samples
    triads = triads / cell_count
    coupling = coupling / cell_count
    weights = pairs - covariance.reshape(extent * extent)[:, None]
    quadratic = lax.dot_general(triads, weights, (((0,), (0,)), ((), ())), precision=FAST)
    new_coefficients = centered + TIME_STEP * (matmul(coupling, centered) + quadratic)
    weighted = matmul(covariance.T, flattened)
    new_mean = mean_flat + TIME_STEP * (
        -mean_flat * mean_gradient + VISCOSITY * mean_smooth - jnp.sum(weighted * gradient, axis=0)
    )
    moment_flat = third_moment.reshape(extent, extent * extent)
    moment_term = fast_matmul(moment_flat, products)
    forcing = matmul(covariance, linear) - moment_term
    half_power = inverse_root(covariance)
    weighting = matmul(half_power, half_power)
    projection = matmul(covariance, coupling.T) + matmul(moment_flat, triads)
    residual = forcing - matmul(projection, flattened)
    stepped = flattened + TIME_STEP * matmul(weighting, residual)
    gram_matrix = doubling_sum(matmul(stepped, stepped.T)) / cell_count
    factor = jnp.linalg.cholesky(gram_matrix)
    new_modes = lax.linalg.triangular_solve(factor, stepped, left_side=True, lower=True)
    return (
        new_modes.reshape(mode_fields.shape),
        new_mean.reshape(mean_field.shape),
        new_coefficients,
    )


def solution(mesh):
    placed = (P(None, "gy", "gx"), P("gy", "gx"), P(None, ("gx", "gy")))
    return jax.shard_map(
        per_device,
        mesh=mesh,
        in_specs=placed,
        out_specs=(P(None, "gy", "gx"), P("gy", "gx"), P(None, ("gx", "gy"))),
        check_vma=False,
    )
```

```python
import jax
import jax.numpy as jnp
import numpy as np
from jax import lax
from jax.sharding import PartitionSpec as P

NS_ITERS = 6


TIME_STEP = 0.02
VISCOSITY = 0.25
PRECISE = lax.Precision.HIGHEST
FAST = lax.Precision.HIGH


AXES = ("gx", "gy")


def device_count():
    return lax.axis_size("gx") * lax.axis_size("gy")


def linear_index():
    return lax.axis_index("gx") * lax.axis_size("gy") + lax.axis_index("gy")


def exchange_bits(reverse=False):
    count = device_count()
    bits = [1 << b for b in range(count.bit_length() - 1)]
    first = lax.axis_size("gy")
    rest = [bit for bit in bits if bit != first]
    return [first] + (rest[::-1] if reverse else rest)


def swap(values, bit):
    count = device_count()
    return lax.ppermute(values, AXES, [(i, i ^ bit) for i in range(count)])


def doubling_sum(values):
    count = device_count()
    if count & (count - 1):
        return lax.psum(values, AXES)
    for bit in exchange_bits():
        values = values + swap(values, bit)
    return values


def halving_sum(parts, reverse=False):
    count = device_count()
    if count & (count - 1):
        return lax.psum(parts, AXES)
    shapes = [part.shape for part in parts]
    flat = jnp.concatenate([part.reshape(-1) for part in parts])
    total = flat.shape[0]
    unit = count * 128
    padded = -(-total // unit) * unit
    flat = jnp.pad(flat, (0, padded - total)).reshape(padded // 128, 128)
    me = linear_index()
    bits = exchange_bits(reverse)
    for bit in bits:
        half = flat.shape[0] // 2
        upper = (me // bit) % 2
        keep = lax.dynamic_slice_in_dim(flat, upper * half, half)
        send = lax.dynamic_slice_in_dim(flat, (1 - upper) * half, half)
        flat = keep + swap(send, bit)
    for bit in reversed(bits):
        upper = (me // bit) % 2
        other = swap(flat, bit)
        both = jnp.zeros((2 * flat.shape[0], 128), flat.dtype)
        both = lax.dynamic_update_slice_in_dim(both, flat, upper * flat.shape[0], 0)
        flat = lax.dynamic_update_slice_in_dim(both, other, (1 - upper) * flat.shape[0], 0)
    flat = flat.reshape(-1)[:total]
    out, start = [], 0
    for shape in shapes:
        size = int(np.prod(shape))
        out.append(flat[start:start + size].reshape(shape))
        start += size
    return out


def padded_2(array, sides, width):
    for axis, dim in sides:
        size, length = (lax.axis_size(axis), array.shape[dim])
        up = [(i, (i + 1) % size) for i in range(size)]
        down = [(j, i) for i, j in up]
        last = lax.slice_in_dim(array, length - width, length, axis=dim)
        first = lax.slice_in_dim(array, 0, width, axis=dim)
        before = lax.ppermute(last, axis, up)
        after = lax.ppermute(first, axis, down)
        array = jnp.concatenate([before, array, after], axis=dim)
    return array


def matmul(left, right):
    return jnp.dot(left, right, precision=PRECISE)


def fast_matmul(left, right):
    return jnp.dot(left, right, precision=FAST)


def pair_index(extent):
    flat_pairs = np.arange(extent * extent)
    leading = flat_pairs // extent
    trailing = flat_pairs % extent
    return (leading, trailing)


def pair_rows(values):
    extent = values.shape[0]
    return (values[:, None, :] * values[None, :, :]).reshape(extent * extent, values.shape[1])


def inverse_root(covariance):
    identity = jnp.eye(covariance.shape[0], dtype=jnp.float32)
    scaling = jnp.sqrt(jnp.sum(covariance * covariance) + 1e-06)
    current = covariance / scaling
    inverse = identity
    for iteration in range(NS_ITERS):
        middle = 0.5 * (3.0 * identity - matmul(inverse, current))
        current = matmul(current, middle)
        inverse = matmul(middle, inverse)
    return inverse / jnp.sqrt(scaling)


def per_device(mode_fields, mean_field, coefficients):
    extent = mode_fields.shape[0]
    devices = lax.axis_size("gx") * lax.axis_size("gy")
    local_cells = mode_fields.shape[1] * mode_fields.shape[2]
    cell_count = local_cells * devices
    samples = coefficients.shape[1] * devices
    stacked = jnp.concatenate([mean_field[None], mode_fields], axis=0)
    padded = padded_2(stacked, (("gx", 2), ("gy", 1)), 1)
    middle = padded[:, 1:-1, 1:-1]
    western = padded[:, 1:-1, :-2]
    eastern = padded[:, 1:-1, 2:]
    southern = padded[:, :-2, 1:-1]
    northern = padded[:, 2:, 1:-1]
    upwinded = (2.0 * middle - western - southern).reshape(extent + 1, local_cells)
    smoothed = (western + eastern + southern + northern - 4.0 * middle).reshape(
        extent + 1, local_cells
    )
    mean_flat = mean_field.reshape(local_cells)
    mean_gradient = upwinded[0]
    mean_smooth = smoothed[0]
    gradient = upwinded[1:]
    flattened = mode_fields.reshape(extent, local_cells)
    linear = -mean_flat * gradient - flattened * mean_gradient + VISCOSITY * smoothed[1:]
    coupling_part = matmul(flattened, linear.T)
    products = (flattened[:, None, :] * gradient[None, :, :]).reshape(extent * extent, local_cells)
    triad_full = -fast_matmul(products, flattened.T)
    totals = doubling_sum(jnp.sum(coefficients, axis=1))
    sample_mean = totals / samples
    centered = coefficients - sample_mean[:, None]
    pairs = pair_rows(centered)
    covariance, third_moment = halving_sum(
        [matmul(centered, centered.T), fast_matmul(pairs, centered.T)]
    )
    triads, coupling = halving_sum([triad_full, coupling_part], reverse=True)
    covariance = covariance / samples
    third_moment = third_moment / samples
    triads = triads / cell_count
    coupling = coupling / cell_count
    weights = pairs - covariance.reshape(extent * extent)[:, None]
    quadratic = lax.dot_general(triads, weights, (((0,), (0,)), ((), ())), precision=FAST)
    new_coefficients = centered + TIME_STEP * (matmul(coupling, centered) + quadratic)
    weighted = matmul(covariance.T, flattened)
    new_mean = mean_flat + TIME_STEP * (
        -mean_flat * mean_gradient + VISCOSITY * mean_smooth - jnp.sum(weighted * gradient, axis=0)
    )
    moment_flat = third_moment.reshape(extent, extent * extent)
    moment_term = fast_matmul(moment_flat, products)
    forcing = matmul(covariance, linear) - moment_term
    half_power = inverse_root(covariance)
    weighting = matmul(half_power, half_power)
    projection = matmul(covariance, coupling.T) + matmul(moment_flat, triads)
    residual = forcing - matmul(projection, flattened)
    stepped = flattened + TIME_STEP * matmul(weighting, residual)
    gram_matrix = doubling_sum(matmul(stepped, stepped.T)) / cell_count
    factor = jnp.linalg.cholesky(gram_matrix)
    new_modes = lax.linalg.triangular_solve(factor, stepped, left_side=True, lower=True)
    return (
        new_modes.reshape(mode_fields.shape),
        new_mean.reshape(mean_field.shape),
        new_coefficients,
    )


def solution(mesh):
    placed = (P(None, "gy", "gx"), P("gy", "gx"), P(None, ("gx", "gy")))
    return jax.shard_map(
        per_device,
        mesh=mesh,
        in_specs=placed,
        out_specs=(P(None, "gy", "gx"), P("gy", "gx"), P(None, ("gx", "gy"))),
        check_vma=False,
    )
```

```python
import jax
import jax.numpy as jnp
import numpy as np
from jax import lax
from jax.sharding import PartitionSpec as P

NS_ITERS = 6


TIME_STEP = 0.02
VISCOSITY = 0.25
PRECISE = lax.Precision.HIGHEST
FAST = lax.Precision.HIGH


AXES = ("gx", "gy")


def device_count():
    return lax.axis_size("gx") * lax.axis_size("gy")


def linear_index():
    return lax.axis_index("gx") * lax.axis_size("gy") + lax.axis_index("gy")


def exchange_bits():
    count = device_count()
    bits = [1 << b for b in range(count.bit_length() - 1)]
    first = lax.axis_size("gy")
    return [first] + [bit for bit in bits if bit != first]


def swap(values, bit):
    count = device_count()
    return lax.ppermute(values, AXES, [(i, i ^ bit) for i in range(count)])


def doubling_sum(values):
    count = device_count()
    if count & (count - 1):
        return lax.psum(values, AXES)
    for bit in exchange_bits():
        values = values + swap(values, bit)
    return values


def halving_sum(parts):
    count = device_count()
    if count & (count - 1):
        return lax.psum(parts, AXES)
    shapes = [part.shape for part in parts]
    flat = jnp.concatenate([part.reshape(-1) for part in parts])
    total = flat.shape[0]
    unit = count * 128
    padded = -(-total // unit) * unit
    flat = jnp.pad(flat, (0, padded - total)).reshape(padded // 128, 128)
    me = linear_index()
    bits = exchange_bits()
    for bit in bits:
        half = flat.shape[0] // 2
        upper = (me // bit) % 2
        keep = lax.dynamic_slice_in_dim(flat, upper * half, half)
        send = lax.dynamic_slice_in_dim(flat, (1 - upper) * half, half)
        flat = keep + swap(send, bit)
    for bit in reversed(bits):
        upper = (me // bit) % 2
        other = swap(flat, bit)
        both = jnp.zeros((2 * flat.shape[0], 128), flat.dtype)
        both = lax.dynamic_update_slice_in_dim(both, flat, upper * flat.shape[0], 0)
        flat = lax.dynamic_update_slice_in_dim(both, other, (1 - upper) * flat.shape[0], 0)
    flat = flat.reshape(-1)[:total]
    out, start = [], 0
    for shape in shapes:
        size = int(np.prod(shape))
        out.append(flat[start:start + size].reshape(shape))
        start += size
    return out


def mirror_masks(half):
    row = lax.broadcasted_iota(jnp.int32, (half, 1, half), 0)
    col = lax.broadcasted_iota(jnp.int32, (half, 1, half), 2)
    return row, col


def pack_mirror(values):
    if values.shape[0] % 2:
        return [values]
    half = values.shape[0] // 2
    row, col = mirror_masks(half)
    upper = values[:half, :, half:]
    lower = values[half:, :, half:]
    merged = jnp.where(row >= col, values[:half, :, :half], lower)
    diagonal = jnp.sum(jnp.where(row == col, lower, 0.0), axis=2)
    return [upper, merged, diagonal]


def unpack_mirror(*parts):
    if len(parts) == 1:
        return parts[0]
    upper, merged, diagonal = parts
    row, col = mirror_masks(merged.shape[0])
    flipped = jnp.transpose(merged, (2, 1, 0))
    first = jnp.where(row >= col, merged, flipped)
    last = jnp.where(row < col, merged, jnp.where(row > col, flipped, diagonal[:, :, None]))
    top = jnp.concatenate([first, upper], axis=2)
    bottom = jnp.concatenate([jnp.transpose(upper, (2, 1, 0)), last], axis=2)
    return jnp.concatenate([top, bottom], axis=0)


def padded_2(array, sides, width):
    for axis, dim in sides:
        size, length = (lax.axis_size(axis), array.shape[dim])
        up = [(i, (i + 1) % size) for i in range(size)]
        down = [(j, i) for i, j in up]
        last = lax.slice_in_dim(array, length - width, length, axis=dim)
        first = lax.slice_in_dim(array, 0, width, axis=dim)
        before = lax.ppermute(last, axis, up)
        after = lax.ppermute(first, axis, down)
        array = jnp.concatenate([before, array, after], axis=dim)
    return array


def matmul(left, right):
    return jnp.dot(left, right, precision=PRECISE)


def fast_matmul(left, right):
    return jnp.dot(left, right, precision=FAST)


def pair_index(extent):
    flat_pairs = np.arange(extent * extent)
    leading = flat_pairs // extent
    trailing = flat_pairs % extent
    return (leading, trailing)


def pair_rows(values):
    extent = values.shape[0]
    return (values[:, None, :] * values[None, :, :]).reshape(extent * extent, values.shape[1])


def inverse_root(covariance):
    identity = jnp.eye(covariance.shape[0], dtype=jnp.float32)
    scaling = jnp.sqrt(jnp.sum(covariance * covariance) + 1e-06)
    current = covariance / scaling
    inverse = identity
    for iteration in range(NS_ITERS):
        middle = 0.5 * (3.0 * identity - matmul(inverse, current))
        current = matmul(current, middle)
        inverse = matmul(middle, inverse)
    return inverse / jnp.sqrt(scaling)


def per_device(mode_fields, mean_field, coefficients):
    extent = mode_fields.shape[0]
    devices = lax.axis_size("gx") * lax.axis_size("gy")
    local_cells = mode_fields.shape[1] * mode_fields.shape[2]
    cell_count = local_cells * devices
    samples = coefficients.shape[1] * devices
    stacked = jnp.concatenate([mean_field[None], mode_fields], axis=0)
    padded = padded_2(stacked, (("gx", 2), ("gy", 1)), 1)
    middle = padded[:, 1:-1, 1:-1]
    western = padded[:, 1:-1, :-2]
    eastern = padded[:, 1:-1, 2:]
    southern = padded[:, :-2, 1:-1]
    northern = padded[:, 2:, 1:-1]
    upwinded = (2.0 * middle - western - southern).reshape(extent + 1, local_cells)
    smoothed = (western + eastern + southern + northern - 4.0 * middle).reshape(
        extent + 1, local_cells
    )
    mean_flat = mean_field.reshape(local_cells)
    mean_gradient = upwinded[0]
    mean_smooth = smoothed[0]
    gradient = upwinded[1:]
    flattened = mode_fields.reshape(extent, local_cells)
    linear = -mean_flat * gradient - flattened * mean_gradient + VISCOSITY * smoothed[1:]
    coupling_part = matmul(flattened, linear.T)
    products = (flattened[:, None, :] * gradient[None, :, :]).reshape(extent * extent, local_cells)
    triad_full = -fast_matmul(products, flattened.T)
    totals = doubling_sum(jnp.sum(coefficients, axis=1))
    sample_mean = totals / samples
    centered = coefficients - sample_mean[:, None]
    pairs = pair_rows(centered)
    cube = (extent, extent, extent)
    covariance, *third_parts = halving_sum(
        [matmul(centered, centered.T)] + pack_mirror(fast_matmul(pairs, centered.T).reshape(cube))
    )
    third_moment = unpack_mirror(*third_parts).reshape(extent * extent, extent)
    coupling, *triad_parts = halving_sum([coupling_part] + pack_mirror(triad_full.reshape(cube)))
    triads = unpack_mirror(*triad_parts).reshape(extent * extent, extent)
    covariance = covariance / samples
    third_moment = third_moment / samples
    triads = triads / cell_count
    coupling = coupling / cell_count
    weights = pairs - covariance.reshape(extent * extent)[:, None]
    quadratic = lax.dot_general(triads, weights, (((0,), (0,)), ((), ())), precision=FAST)
    new_coefficients = centered + TIME_STEP * (matmul(coupling, centered) + quadratic)
    weighted = matmul(covariance.T, flattened)
    new_mean = mean_flat + TIME_STEP * (
        -mean_flat * mean_gradient + VISCOSITY * mean_smooth - jnp.sum(weighted * gradient, axis=0)
    )
    moment_flat = third_moment.reshape(extent, extent * extent)
    moment_term = fast_matmul(moment_flat, products)
    forcing = matmul(covariance, linear) - moment_term
    half_power = inverse_root(covariance)
    weighting = matmul(half_power, half_power)
    projection = matmul(covariance, coupling.T) + matmul(moment_flat, triads)
    residual = forcing - matmul(projection, flattened)
    stepped = flattened + TIME_STEP * matmul(weighting, residual)
    gram_matrix = doubling_sum(matmul(stepped, stepped.T)) / cell_count
    factor = jnp.linalg.cholesky(gram_matrix)
    new_modes = lax.linalg.triangular_solve(factor, stepped, left_side=True, lower=True)
    return (
        new_modes.reshape(mode_fields.shape),
        new_mean.reshape(mean_field.shape),
        new_coefficients,
    )


def solution(mesh):
    placed = (P(None, "gy", "gx"), P("gy", "gx"), P(None, ("gx", "gy")))
    return jax.shard_map(
        per_device,
        mesh=mesh,
        in_specs=placed,
        out_specs=(P(None, "gy", "gx"), P("gy", "gx"), P(None, ("gx", "gy"))),
        check_vma=False,
    )
```

```python
import jax
import jax.numpy as jnp
import numpy as np
from jax import lax
from jax.sharding import PartitionSpec as P

NS_ITERS = 6


TIME_STEP = 0.02
VISCOSITY = 0.25
PRECISE = lax.Precision.HIGHEST
FAST = lax.Precision.HIGH


AXES = ("gx", "gy")


def device_count():
    return lax.axis_size("gx") * lax.axis_size("gy")


def linear_index():
    return lax.axis_index("gx") * lax.axis_size("gy") + lax.axis_index("gy")


def exchange_bits():
    count = device_count()
    bits = [1 << b for b in range(count.bit_length() - 1)]
    first = lax.axis_size("gy")
    return [first] + [bit for bit in bits if bit != first]


def swap(values, bit):
    count = device_count()
    return lax.ppermute(values, AXES, [(i, i ^ bit) for i in range(count)])


def doubling_sum(values):
    count = device_count()
    if count & (count - 1):
        return lax.psum(values, AXES)
    for bit in exchange_bits():
        values = values + swap(values, bit)
    return values


def halving_sum(parts):
    count = device_count()
    if count & (count - 1):
        return lax.psum(parts, AXES)
    shapes = [part.shape for part in parts]
    flat = jnp.concatenate([part.reshape(-1) for part in parts])
    total = flat.shape[0]
    unit = count * 128
    padded = -(-total // unit) * unit
    flat = jnp.pad(flat, (0, padded - total)).reshape(padded // 128, 128)
    me = linear_index()
    bits = exchange_bits()
    for bit in bits:
        half = flat.shape[0] // 2
        upper = (me // bit) % 2
        keep = lax.dynamic_slice_in_dim(flat, upper * half, half)
        send = lax.dynamic_slice_in_dim(flat, (1 - upper) * half, half)
        flat = keep + swap(send, bit)
    for bit in reversed(bits):
        upper = (me // bit) % 2
        other = swap(flat, bit)
        both = jnp.zeros((2 * flat.shape[0], 128), flat.dtype)
        both = lax.dynamic_update_slice_in_dim(both, flat, upper * flat.shape[0], 0)
        flat = lax.dynamic_update_slice_in_dim(both, other, (1 - upper) * flat.shape[0], 0)
    flat = flat.reshape(-1)[:total]
    out, start = [], 0
    for shape in shapes:
        size = int(np.prod(shape))
        out.append(flat[start:start + size].reshape(shape))
        start += size
    return out


def mirror_masks(half):
    row = lax.broadcasted_iota(jnp.int32, (half, half, 1), 0)
    col = lax.broadcasted_iota(jnp.int32, (half, half, 1), 1)
    return row, col


def pack_mirror(values):
    if values.shape[0] % 2:
        return [values]
    half = values.shape[0] // 2
    row, col = mirror_masks(half)
    upper = values[:half, half:]
    lower = values[half:, half:]
    merged = jnp.where(row >= col, values[:half, :half], lower)
    diagonal = jnp.sum(jnp.where(row == col, lower, 0.0), axis=1)
    return [upper, merged, diagonal]


def unpack_mirror(*parts):
    if len(parts) == 1:
        return parts[0]
    upper, merged, diagonal = parts
    row, col = mirror_masks(merged.shape[0])
    flipped = jnp.transpose(merged, (1, 0, 2))
    first = jnp.where(row >= col, merged, flipped)
    last = jnp.where(row < col, merged, jnp.where(row > col, flipped, diagonal[:, None, :]))
    top = jnp.concatenate([first, upper], axis=1)
    bottom = jnp.concatenate([jnp.transpose(upper, (1, 0, 2)), last], axis=1)
    return jnp.concatenate([top, bottom], axis=0)


def padded_2(array, sides, width):
    for axis, dim in sides:
        size, length = (lax.axis_size(axis), array.shape[dim])
        up = [(i, (i + 1) % size) for i in range(size)]
        down = [(j, i) for i, j in up]
        last = lax.slice_in_dim(array, length - width, length, axis=dim)
        first = lax.slice_in_dim(array, 0, width, axis=dim)
        before = lax.ppermute(last, axis, up)
        after = lax.ppermute(first, axis, down)
        array = jnp.concatenate([before, array, after], axis=dim)
    return array


def matmul(left, right):
    return jnp.dot(left, right, precision=PRECISE)


def fast_matmul(left, right):
    return jnp.dot(left, right, precision=FAST)


def pair_index(extent):
    flat_pairs = np.arange(extent * extent)
    leading = flat_pairs // extent
    trailing = flat_pairs % extent
    return (leading, trailing)


def pair_rows(values):
    extent = values.shape[0]
    return (values[:, None, :] * values[None, :, :]).reshape(extent * extent, values.shape[1])


def inverse_root(covariance):
    identity = jnp.eye(covariance.shape[0], dtype=jnp.float32)
    scaling = jnp.sqrt(jnp.sum(covariance * covariance) + 1e-06)
    current = covariance / scaling
    inverse = identity
    for iteration in range(NS_ITERS):
        middle = 0.5 * (3.0 * identity - matmul(inverse, current))
        current = matmul(current, middle)
        inverse = matmul(middle, inverse)
    return inverse / jnp.sqrt(scaling)


def per_device(mode_fields, mean_field, coefficients):
    extent = mode_fields.shape[0]
    devices = lax.axis_size("gx") * lax.axis_size("gy")
    local_cells = mode_fields.shape[1] * mode_fields.shape[2]
    cell_count = local_cells * devices
    samples = coefficients.shape[1] * devices
    stacked = jnp.concatenate([mean_field[None], mode_fields], axis=0)
    padded = padded_2(stacked, (("gx", 2), ("gy", 1)), 1)
    middle = padded[:, 1:-1, 1:-1]
    western = padded[:, 1:-1, :-2]
    eastern = padded[:, 1:-1, 2:]
    southern = padded[:, :-2, 1:-1]
    northern = padded[:, 2:, 1:-1]
    upwinded = (2.0 * middle - western - southern).reshape(extent + 1, local_cells)
    smoothed = (western + eastern + southern + northern - 4.0 * middle).reshape(
        extent + 1, local_cells
    )
    mean_flat = mean_field.reshape(local_cells)
    mean_gradient = upwinded[0]
    mean_smooth = smoothed[0]
    gradient = upwinded[1:]
    flattened = mode_fields.reshape(extent, local_cells)
    linear = -mean_flat * gradient - flattened * mean_gradient + VISCOSITY * smoothed[1:]
    coupling_part = matmul(flattened, linear.T)
    products = (flattened[:, None, :] * gradient[None, :, :]).reshape(extent * extent, local_cells)
    triad_rows = -fast_matmul(flattened, products.T)
    totals = doubling_sum(jnp.sum(coefficients, axis=1))
    sample_mean = totals / samples
    centered = coefficients - sample_mean[:, None]
    pairs = pair_rows(centered)
    cube = (extent, extent, extent)
    covariance, *third_parts = halving_sum(
        [matmul(centered, centered.T)] + pack_mirror(fast_matmul(pairs, centered.T).reshape(cube))
    )
    third_moment = unpack_mirror(*third_parts).reshape(extent * extent, extent)
    coupling, *triad_parts = halving_sum([coupling_part] + pack_mirror(triad_rows.reshape(cube)))
    triads = unpack_mirror(*triad_parts).reshape(extent, extent * extent)
    covariance = covariance / samples
    third_moment = third_moment / samples
    triads = triads / cell_count
    coupling = coupling / cell_count
    weights = pairs - covariance.reshape(extent * extent)[:, None]
    quadratic = jnp.dot(triads, weights, precision=FAST)
    new_coefficients = centered + TIME_STEP * (matmul(coupling, centered) + quadratic)
    weighted = matmul(covariance.T, flattened)
    new_mean = mean_flat + TIME_STEP * (
        -mean_flat * mean_gradient + VISCOSITY * mean_smooth - jnp.sum(weighted * gradient, axis=0)
    )
    moment_flat = third_moment.reshape(extent, extent * extent)
    moment_term = fast_matmul(moment_flat, products)
    forcing = matmul(covariance, linear) - moment_term
    half_power = inverse_root(covariance)
    weighting = matmul(half_power, half_power)
    projection = matmul(covariance, coupling.T) + matmul(moment_flat, triads.T)
    residual = forcing - matmul(projection, flattened)
    stepped = flattened + TIME_STEP * matmul(weighting, residual)
    gram_matrix = doubling_sum(matmul(stepped, stepped.T)) / cell_count
    factor = jnp.linalg.cholesky(gram_matrix)
    new_modes = lax.linalg.triangular_solve(factor, stepped, left_side=True, lower=True)
    return (
        new_modes.reshape(mode_fields.shape),
        new_mean.reshape(mean_field.shape),
        new_coefficients,
    )


def solution(mesh):
    placed = (P(None, "gy", "gx"), P("gy", "gx"), P(None, ("gx", "gy")))
    return jax.shard_map(
        per_device,
        mesh=mesh,
        in_specs=placed,
        out_specs=(P(None, "gy", "gx"), P("gy", "gx"), P(None, ("gx", "gy"))),
        check_vma=False,
    )
```

```python
import jax
import jax.numpy as jnp
import numpy as np
from jax import lax
from jax.sharding import PartitionSpec as P

NS_ITERS = 6


TIME_STEP = 0.02
VISCOSITY = 0.25
PRECISE = lax.Precision.HIGHEST
FAST = lax.Precision.HIGH


AXES = ("gx", "gy")


def device_count():
    return lax.axis_size("gx") * lax.axis_size("gy")


def linear_index():
    return lax.axis_index("gx") * lax.axis_size("gy") + lax.axis_index("gy")


def exchange_bits():
    count = device_count()
    bits = [1 << b for b in range(count.bit_length() - 1)]
    first = lax.axis_size("gy")
    return [first] + [bit for bit in bits if bit != first]


def swap(values, bit):
    count = device_count()
    return lax.ppermute(values, AXES, [(i, i ^ bit) for i in range(count)])


def doubling_sum(values):
    count = device_count()
    if count & (count - 1):
        return lax.psum(values, AXES)
    for bit in exchange_bits():
        values = values + swap(values, bit)
    return values


def halving_sum(parts):
    count = device_count()
    if count & (count - 1):
        return lax.psum(parts, AXES)
    shapes = [part.shape for part in parts]
    flat = jnp.concatenate([part.reshape(-1) for part in parts])
    total = flat.shape[0]
    unit = count * 128
    padded = -(-total // unit) * unit
    flat = jnp.pad(flat, (0, padded - total)).reshape(padded // 128, 128)
    me = linear_index()
    bits = exchange_bits()
    for bit in bits:
        half = flat.shape[0] // 2
        upper = (me // bit) % 2
        keep = lax.dynamic_slice_in_dim(flat, upper * half, half)
        send = lax.dynamic_slice_in_dim(flat, (1 - upper) * half, half)
        flat = keep + swap(send, bit)
    for bit in reversed(bits):
        upper = (me // bit) % 2
        other = swap(flat, bit)
        both = jnp.zeros((2 * flat.shape[0], 128), flat.dtype)
        both = lax.dynamic_update_slice_in_dim(both, flat, upper * flat.shape[0], 0)
        flat = lax.dynamic_update_slice_in_dim(both, other, (1 - upper) * flat.shape[0], 0)
    flat = flat.reshape(-1)[:total]
    out, start = [], 0
    for shape in shapes:
        size = int(np.prod(shape))
        out.append(flat[start:start + size].reshape(shape))
        start += size
    return out


def mirror_masks(half):
    row = lax.broadcasted_iota(jnp.int32, (half, half, 1), 0)
    col = lax.broadcasted_iota(jnp.int32, (half, half, 1), 1)
    return row, col


def pack_mirror(values):
    if values.shape[0] % 2:
        return [values]
    half = values.shape[0] // 2
    row, col = mirror_masks(half)
    upper = values[:half, half:]
    lower = values[half:, half:]
    merged = jnp.where(row >= col, values[:half, :half], lower)
    diagonal = jnp.sum(jnp.where(row == col, lower, 0.0), axis=1)
    return [upper, merged, diagonal]


def unpack_mirror(*parts):
    if len(parts) == 1:
        return parts[0]
    upper, merged, diagonal = parts
    row, col = mirror_masks(merged.shape[0])
    flipped = jnp.transpose(merged, (1, 0, 2))
    first = jnp.where(row >= col, merged, flipped)
    last = jnp.where(row < col, merged, jnp.where(row > col, flipped, diagonal[:, None, :]))
    top = jnp.concatenate([first, upper], axis=1)
    bottom = jnp.concatenate([jnp.transpose(upper, (1, 0, 2)), last], axis=1)
    return jnp.concatenate([top, bottom], axis=0)


def shift_pair(array, axis, dim):
    size, length = (lax.axis_size(axis), array.shape[dim])
    up = [(i, (i + 1) % size) for i in range(size)]
    down = [(j, i) for i, j in up]
    last = lax.slice_in_dim(array, length - 1, length, axis=dim)
    first = lax.slice_in_dim(array, 0, 1, axis=dim)
    return lax.ppermute(last, axis, up), lax.ppermute(first, axis, down)


def padded_cross(array):
    west, east = shift_pair(array, "gx", 2)
    south, north = shift_pair(array, "gy", 1)
    middle = jnp.concatenate([west, array, east], axis=2)
    corners = ((0, 0), (0, 0), (1, 1))
    return jnp.concatenate([jnp.pad(south, corners), middle, jnp.pad(north, corners)], axis=1)


def matmul(left, right):
    return jnp.dot(left, right, precision=PRECISE)


def fast_matmul(left, right):
    return jnp.dot(left, right, precision=FAST)


def pair_index(extent):
    flat_pairs = np.arange(extent * extent)
    leading = flat_pairs // extent
    trailing = flat_pairs % extent
    return (leading, trailing)


def pair_rows(values):
    extent = values.shape[0]
    return (values[:, None, :] * values[None, :, :]).reshape(extent * extent, values.shape[1])


def inverse_root(covariance):
    identity = jnp.eye(covariance.shape[0], dtype=jnp.float32)
    scaling = jnp.sqrt(jnp.sum(covariance * covariance) + 1e-06)
    current = covariance / scaling
    inverse = identity
    for iteration in range(NS_ITERS):
        middle = 0.5 * (3.0 * identity - matmul(inverse, current))
        current = matmul(current, middle)
        inverse = matmul(middle, inverse)
    return inverse / jnp.sqrt(scaling)


def per_device(mode_fields, mean_field, coefficients):
    extent = mode_fields.shape[0]
    devices = lax.axis_size("gx") * lax.axis_size("gy")
    local_cells = mode_fields.shape[1] * mode_fields.shape[2]
    cell_count = local_cells * devices
    samples = coefficients.shape[1] * devices
    stacked = jnp.concatenate([mean_field[None], mode_fields], axis=0)
    padded = padded_cross(stacked)
    middle = padded[:, 1:-1, 1:-1]
    western = padded[:, 1:-1, :-2]
    eastern = padded[:, 1:-1, 2:]
    southern = padded[:, :-2, 1:-1]
    northern = padded[:, 2:, 1:-1]
    upwinded = (2.0 * middle - western - southern).reshape(extent + 1, local_cells)
    smoothed = (western + eastern + southern + northern - 4.0 * middle).reshape(
        extent + 1, local_cells
    )
    mean_flat = mean_field.reshape(local_cells)
    mean_gradient = upwinded[0]
    mean_smooth = smoothed[0]
    gradient = upwinded[1:]
    flattened = mode_fields.reshape(extent, local_cells)
    linear = -mean_flat * gradient - flattened * mean_gradient + VISCOSITY * smoothed[1:]
    coupling_part = matmul(flattened, linear.T)
    products = (flattened[:, None, :] * gradient[None, :, :]).reshape(extent * extent, local_cells)
    triad_rows = -fast_matmul(flattened, products.T)
    totals = doubling_sum(jnp.sum(coefficients, axis=1))
    sample_mean = totals / samples
    centered = coefficients - sample_mean[:, None]
    pairs = pair_rows(centered)
    cube = (extent, extent, extent)
    covariance, *third_parts = halving_sum(
        [matmul(centered, centered.T)] + pack_mirror(fast_matmul(pairs, centered.T).reshape(cube))
    )
    third_moment = unpack_mirror(*third_parts).reshape(extent * extent, extent)
    coupling, *triad_parts = halving_sum([coupling_part] + pack_mirror(triad_rows.reshape(cube)))
    triads = unpack_mirror(*triad_parts).reshape(extent, extent * extent)
    covariance = covariance / samples
    third_moment = third_moment / samples
    triads = triads / cell_count
    coupling = coupling / cell_count
    weights = pairs - covariance.reshape(extent * extent)[:, None]
    quadratic = jnp.dot(triads, weights, precision=FAST)
    new_coefficients = centered + TIME_STEP * (matmul(coupling, centered) + quadratic)
    weighted = matmul(covariance.T, flattened)
    new_mean = mean_flat + TIME_STEP * (
        -mean_flat * mean_gradient + VISCOSITY * mean_smooth - jnp.sum(weighted * gradient, axis=0)
    )
    moment_flat = third_moment.reshape(extent, extent * extent)
    moment_term = fast_matmul(moment_flat, products)
    forcing = matmul(covariance, linear) - moment_term
    half_power = inverse_root(covariance)
    weighting = matmul(half_power, half_power)
    projection = matmul(covariance, coupling.T) + matmul(moment_flat, triads.T)
    residual = forcing - matmul(projection, flattened)
    stepped = flattened + TIME_STEP * matmul(weighting, residual)
    gram_matrix = doubling_sum(matmul(stepped, stepped.T)) / cell_count
    factor = jnp.linalg.cholesky(gram_matrix)
    new_modes = lax.linalg.triangular_solve(factor, stepped, left_side=True, lower=True)
    return (
        new_modes.reshape(mode_fields.shape),
        new_mean.reshape(mean_field.shape),
        new_coefficients,
    )


def solution(mesh):
    placed = (P(None, "gy", "gx"), P("gy", "gx"), P(None, ("gx", "gy")))
    return jax.shard_map(
        per_device,
        mesh=mesh,
        in_specs=placed,
        out_specs=(P(None, "gy", "gx"), P("gy", "gx"), P(None, ("gx", "gy"))),
        check_vma=False,
    )
```

```python
import jax
import jax.numpy as jnp
import numpy as np
from jax import lax
from jax.sharding import PartitionSpec as P

NS_ITERS = 6


TIME_STEP = 0.02
VISCOSITY = 0.25
PRECISE = lax.Precision.HIGHEST
FAST = lax.Precision.HIGH


AXES = ("gx", "gy")


def device_count():
    return lax.axis_size("gx") * lax.axis_size("gy")


def linear_index():
    return lax.axis_index("gx") * lax.axis_size("gy") + lax.axis_index("gy")


def exchange_bits():
    count = device_count()
    bits = [1 << b for b in range(count.bit_length() - 1)]
    first = lax.axis_size("gy")
    return [first] + [bit for bit in bits if bit != first]


def swap(values, bit):
    count = device_count()
    return lax.ppermute(values, AXES, [(i, i ^ bit) for i in range(count)])


def doubling_sum(values):
    count = device_count()
    if count & (count - 1):
        return lax.psum(values, AXES)
    for bit in exchange_bits():
        values = values + swap(values, bit)
    return values


def halving_sum(parts):
    count = device_count()
    if count & (count - 1):
        return lax.psum(parts, AXES)
    shapes = [part.shape for part in parts]
    flat = jnp.concatenate([part.reshape(-1) for part in parts])
    total = flat.shape[0]
    unit = count * 128
    padded = -(-total // unit) * unit
    flat = jnp.pad(flat, (0, padded - total)).reshape(padded // 128, 128)
    me = linear_index()
    bits = exchange_bits()
    for bit in bits:
        half = flat.shape[0] // 2
        upper = (me // bit) % 2
        keep = lax.dynamic_slice_in_dim(flat, upper * half, half)
        send = lax.dynamic_slice_in_dim(flat, (1 - upper) * half, half)
        flat = keep + swap(send, bit)
    for bit in reversed(bits):
        upper = (me // bit) % 2
        other = swap(flat, bit)
        both = jnp.zeros((2 * flat.shape[0], 128), flat.dtype)
        both = lax.dynamic_update_slice_in_dim(both, flat, upper * flat.shape[0], 0)
        flat = lax.dynamic_update_slice_in_dim(both, other, (1 - upper) * flat.shape[0], 0)
    flat = flat.reshape(-1)[:total]
    out, start = [], 0
    for shape in shapes:
        size = int(np.prod(shape))
        out.append(flat[start:start + size].reshape(shape))
        start += size
    return out


def mirror_masks(half):
    row = lax.broadcasted_iota(jnp.int32, (half, half, 1), 0)
    col = lax.broadcasted_iota(jnp.int32, (half, half, 1), 1)
    return row, col


def pack_mirror(values):
    if values.shape[0] % 2:
        return [values]
    half = values.shape[0] // 2
    row, col = mirror_masks(half)
    upper = values[:half, half:]
    lower = values[half:, half:]
    merged = jnp.where(row >= col, values[:half, :half], lower)
    diagonal = jnp.sum(jnp.where(row == col, lower, 0.0), axis=1)
    return [upper, merged, diagonal]


def unpack_mirror(*parts):
    if len(parts) == 1:
        return parts[0]
    upper, merged, diagonal = parts
    row, col = mirror_masks(merged.shape[0])
    flipped = jnp.transpose(merged, (1, 0, 2))
    first = jnp.where(row >= col, merged, flipped)
    last = jnp.where(row < col, merged, jnp.where(row > col, flipped, diagonal[:, None, :]))
    top = jnp.concatenate([first, upper], axis=1)
    bottom = jnp.concatenate([jnp.transpose(upper, (1, 0, 2)), last], axis=1)
    return jnp.concatenate([top, bottom], axis=0)


def shift_pair(array, axis, dim):
    size, length = (lax.axis_size(axis), array.shape[dim])
    up = [(i, (i + 1) % size) for i in range(size)]
    down = [(j, i) for i, j in up]
    last = lax.slice_in_dim(array, length - 1, length, axis=dim)
    first = lax.slice_in_dim(array, 0, 1, axis=dim)
    return lax.ppermute(last, axis, up), lax.ppermute(first, axis, down)


def padded_cross(array):
    west, east = shift_pair(array, "gx", 2)
    south, north = shift_pair(array, "gy", 1)
    middle = jnp.concatenate([west, array, east], axis=2)
    corners = ((0, 0), (0, 0), (1, 1))
    return jnp.concatenate([jnp.pad(south, corners), middle, jnp.pad(north, corners)], axis=1)


def matmul(left, right):
    return jnp.dot(left, right, precision=PRECISE)


def fast_matmul(left, right):
    return jnp.dot(left, right, precision=FAST)


def pair_index(extent):
    flat_pairs = np.arange(extent * extent)
    leading = flat_pairs // extent
    trailing = flat_pairs % extent
    return (leading, trailing)


def pair_rows(values):
    extent = values.shape[0]
    return (values[:, None, :] * values[None, :, :]).reshape(extent * extent, values.shape[1])


def inverse_root(covariance):
    identity = jnp.eye(covariance.shape[0], dtype=jnp.float32)
    scaling = jnp.sqrt(jnp.sum(covariance * covariance) + 1e-06)
    current = covariance / scaling
    inverse = identity
    for iteration in range(NS_ITERS):
        middle = 0.5 * (3.0 * identity - matmul(inverse, current))
        current = matmul(current, middle)
        inverse = matmul(middle, inverse)
    return inverse / jnp.sqrt(scaling)


def per_device(mode_fields, mean_field, coefficients):
    extent = mode_fields.shape[0]
    devices = lax.axis_size("gx") * lax.axis_size("gy")
    local_cells = mode_fields.shape[1] * mode_fields.shape[2]
    cell_count = local_cells * devices
    samples = coefficients.shape[1] * devices
    stacked = jnp.concatenate([mean_field[None], mode_fields], axis=0)
    padded = padded_cross(stacked)
    middle = padded[:, 1:-1, 1:-1]
    western = padded[:, 1:-1, :-2]
    eastern = padded[:, 1:-1, 2:]
    southern = padded[:, :-2, 1:-1]
    northern = padded[:, 2:, 1:-1]
    upwinded = (2.0 * middle - western - southern).reshape(extent + 1, local_cells)
    smoothed = (western + eastern + southern + northern - 4.0 * middle).reshape(
        extent + 1, local_cells
    )
    mean_flat = mean_field.reshape(local_cells)
    mean_gradient = upwinded[0]
    mean_smooth = smoothed[0]
    gradient = upwinded[1:]
    flattened = mode_fields.reshape(extent, local_cells)
    linear = -mean_flat * gradient - flattened * mean_gradient + VISCOSITY * smoothed[1:]
    coupling_part = matmul(flattened, linear.T)
    local_totals = jnp.sum(coefficients, axis=1)
    count = device_count()
    bits = exchange_bits() if count & (count - 1) == 0 else []
    pieces = max(len(bits), 1)
    bounds = [round(extent * p / pieces) for p in range(pieces + 1)]
    product_chunks, triad_chunks = [], []
    totals = local_totals
    for piece in range(pieces):
        if piece > 0:
            totals = totals + 0.0 * triad_chunks[-1][0, 0]
        if bits:
            received = swap(totals, bits[piece])
        lead = flattened[bounds[piece]:bounds[piece + 1]] + 0.0 * totals[0]
        chunk = (lead[:, None, :] * gradient[None, :, :]).reshape(-1, local_cells)
        product_chunks.append(chunk)
        triad_chunks.append(-fast_matmul(flattened, chunk.T))
        if bits:
            totals = totals + received
    if not bits:
        totals = lax.psum(totals, AXES)
    triad_rows = jnp.concatenate(triad_chunks, axis=1)
    sample_mean = totals / samples
    centered = coefficients - sample_mean[:, None]
    pairs = pair_rows(centered)
    cube = (extent, extent, extent)
    covariance, *third_parts = halving_sum(
        [matmul(centered, centered.T)] + pack_mirror(fast_matmul(pairs, centered.T).reshape(cube))
    )
    third_moment = unpack_mirror(*third_parts).reshape(extent * extent, extent)
    coupling, *triad_parts = halving_sum([coupling_part] + pack_mirror(triad_rows.reshape(cube)))
    triads = unpack_mirror(*triad_parts).reshape(extent, extent * extent)
    covariance = covariance / samples
    third_moment = third_moment / samples
    triads = triads / cell_count
    coupling = coupling / cell_count
    weights = pairs - covariance.reshape(extent * extent)[:, None]
    quadratic = jnp.dot(triads, weights, precision=FAST)
    new_coefficients = centered + TIME_STEP * (matmul(coupling, centered) + quadratic)
    weighted = matmul(covariance.T, flattened)
    new_mean = mean_flat + TIME_STEP * (
        -mean_flat * mean_gradient + VISCOSITY * mean_smooth - jnp.sum(weighted * gradient, axis=0)
    )
    moment_flat = third_moment.reshape(extent, extent * extent)
    moment_term = sum(
        fast_matmul(moment_flat[:, bounds[p] * extent:bounds[p + 1] * extent], product_chunks[p])
        for p in range(pieces)
    )
    forcing = matmul(covariance, linear) - moment_term
    half_power = inverse_root(covariance)
    weighting = matmul(half_power, half_power)
    projection = matmul(covariance, coupling.T) + matmul(moment_flat, triads.T)
    residual = forcing - matmul(projection, flattened)
    stepped = flattened + TIME_STEP * matmul(weighting, residual)
    gram_matrix = doubling_sum(matmul(stepped, stepped.T)) / cell_count
    factor = jnp.linalg.cholesky(gram_matrix)
    new_modes = lax.linalg.triangular_solve(factor, stepped, left_side=True, lower=True)
    return (
        new_modes.reshape(mode_fields.shape),
        new_mean.reshape(mean_field.shape),
        new_coefficients,
    )


def solution(mesh):
    placed = (P(None, "gy", "gx"), P("gy", "gx"), P(None, ("gx", "gy")))
    return jax.shard_map(
        per_device,
        mesh=mesh,
        in_specs=placed,
        out_specs=(P(None, "gy", "gx"), P("gy", "gx"), P(None, ("gx", "gy"))),
        check_vma=False,
    )
```

```python
import jax
import jax.numpy as jnp
import numpy as np
from jax import lax
from jax.sharding import PartitionSpec as P

NS_ITERS = 6


TIME_STEP = 0.02
VISCOSITY = 0.25
PRECISE = lax.Precision.HIGHEST
FAST = lax.Precision.HIGH


AXES = ("gx", "gy")


def device_count():
    return lax.axis_size("gx") * lax.axis_size("gy")


def linear_index():
    return lax.axis_index("gx") * lax.axis_size("gy") + lax.axis_index("gy")


def exchange_bits():
    count = device_count()
    bits = [1 << b for b in range(count.bit_length() - 1)]
    first = lax.axis_size("gy")
    return [first] + [bit for bit in bits if bit != first]


def swap(values, bit):
    count = device_count()
    return lax.ppermute(values, AXES, [(i, i ^ bit) for i in range(count)])


def doubling_sum(values):
    count = device_count()
    if count & (count - 1):
        return lax.psum(values, AXES)
    for bit in exchange_bits():
        values = values + swap(values, bit)
    return values


def halving_sum(parts):
    count = device_count()
    if count & (count - 1):
        return lax.psum(parts, AXES)
    shapes = [part.shape for part in parts]
    flat = jnp.concatenate([part.reshape(-1) for part in parts])
    total = flat.shape[0]
    unit = count * 128
    padded = -(-total // unit) * unit
    flat = jnp.pad(flat, (0, padded - total)).reshape(padded // 128, 128)
    me = linear_index()
    bits = exchange_bits()
    for bit in bits:
        half = flat.shape[0] // 2
        upper = (me // bit) % 2
        keep = lax.dynamic_slice_in_dim(flat, upper * half, half)
        send = lax.dynamic_slice_in_dim(flat, (1 - upper) * half, half)
        flat = keep + swap(send, bit)
    for bit in reversed(bits):
        upper = (me // bit) % 2
        other = swap(flat, bit)
        both = jnp.zeros((2 * flat.shape[0], 128), flat.dtype)
        both = lax.dynamic_update_slice_in_dim(both, flat, upper * flat.shape[0], 0)
        flat = lax.dynamic_update_slice_in_dim(both, other, (1 - upper) * flat.shape[0], 0)
    flat = flat.reshape(-1)[:total]
    out, start = [], 0
    for shape in shapes:
        size = int(np.prod(shape))
        out.append(flat[start:start + size].reshape(shape))
        start += size
    return out


def mirror_masks(half):
    row = lax.broadcasted_iota(jnp.int32, (half, half, 1), 0)
    col = lax.broadcasted_iota(jnp.int32, (half, half, 1), 1)
    return row, col


def pack_mirror(values):
    if values.shape[0] % 2:
        return [values]
    half = values.shape[0] // 2
    row, col = mirror_masks(half)
    upper = values[:half, half:]
    lower = values[half:, half:]
    merged = jnp.where(row >= col, values[:half, :half], lower)
    diagonal = jnp.sum(jnp.where(row == col, lower, 0.0), axis=1)
    return [upper, merged, diagonal]


def unpack_mirror(*parts):
    if len(parts) == 1:
        return parts[0]
    upper, merged, diagonal = parts
    row, col = mirror_masks(merged.shape[0])
    flipped = jnp.transpose(merged, (1, 0, 2))
    first = jnp.where(row >= col, merged, flipped)
    last = jnp.where(row < col, merged, jnp.where(row > col, flipped, diagonal[:, None, :]))
    top = jnp.concatenate([first, upper], axis=1)
    bottom = jnp.concatenate([jnp.transpose(upper, (1, 0, 2)), last], axis=1)
    return jnp.concatenate([top, bottom], axis=0)


def shift_pair(array, axis, dim):
    size, length = (lax.axis_size(axis), array.shape[dim])
    up = [(i, (i + 1) % size) for i in range(size)]
    down = [(j, i) for i, j in up]
    last = lax.slice_in_dim(array, length - 1, length, axis=dim)
    first = lax.slice_in_dim(array, 0, 1, axis=dim)
    return lax.ppermute(last, axis, up), lax.ppermute(first, axis, down)


def padded_cross(array):
    west, east = shift_pair(array, "gx", 2)
    south, north = shift_pair(array, "gy", 1)
    middle = jnp.concatenate([west, array, east], axis=2)
    corners = ((0, 0), (0, 0), (1, 1))
    return jnp.concatenate([jnp.pad(south, corners), middle, jnp.pad(north, corners)], axis=1)


def matmul(left, right):
    return jnp.dot(left, right, precision=PRECISE)


def fast_matmul(left, right):
    return jnp.dot(left, right, precision=FAST)


def pair_index(extent):
    flat_pairs = np.arange(extent * extent)
    leading = flat_pairs // extent
    trailing = flat_pairs % extent
    return (leading, trailing)


def pair_rows(values):
    extent = values.shape[0]
    return (values[:, None, :] * values[None, :, :]).reshape(extent * extent, values.shape[1])


def inverse_root(covariance):
    identity = jnp.eye(covariance.shape[0], dtype=jnp.float32)
    scaling = jnp.sqrt(jnp.sum(covariance * covariance) + 1e-06)
    current = covariance / scaling
    inverse = identity
    for iteration in range(NS_ITERS):
        middle = 0.5 * (3.0 * identity - matmul(inverse, current))
        current = matmul(current, middle)
        inverse = matmul(middle, inverse)
    return inverse / jnp.sqrt(scaling)


def per_device(mode_fields, mean_field, coefficients):
    extent = mode_fields.shape[0]
    devices = lax.axis_size("gx") * lax.axis_size("gy")
    local_cells = mode_fields.shape[1] * mode_fields.shape[2]
    cell_count = local_cells * devices
    samples = coefficients.shape[1] * devices
    stacked = jnp.concatenate([mean_field[None], mode_fields], axis=0)
    padded = padded_cross(stacked)
    middle = padded[:, 1:-1, 1:-1]
    western = padded[:, 1:-1, :-2]
    eastern = padded[:, 1:-1, 2:]
    southern = padded[:, :-2, 1:-1]
    northern = padded[:, 2:, 1:-1]
    upwinded = (2.0 * middle - western - southern).reshape(extent + 1, local_cells)
    smoothed = (western + eastern + southern + northern - 4.0 * middle).reshape(
        extent + 1, local_cells
    )
    mean_flat = mean_field.reshape(local_cells)
    mean_gradient = upwinded[0]
    mean_smooth = smoothed[0]
    gradient = upwinded[1:]
    flattened = mode_fields.reshape(extent, local_cells)
    linear = -mean_flat * gradient - flattened * mean_gradient + VISCOSITY * smoothed[1:]
    coupling_part = fast_matmul(flattened, linear.T)
    products = (flattened[:, None, :] * gradient[None, :, :]).reshape(extent * extent, local_cells)
    triad_rows = -fast_matmul(flattened, products.T)
    totals = doubling_sum(jnp.sum(coefficients, axis=1))
    sample_mean = totals / samples
    centered = coefficients - sample_mean[:, None]
    pairs = pair_rows(centered)
    cube = (extent, extent, extent)
    covariance, *third_parts = halving_sum(
        [matmul(centered, centered.T)] + pack_mirror(fast_matmul(pairs, centered.T).reshape(cube))
    )
    third_moment = unpack_mirror(*third_parts).reshape(extent * extent, extent)
    coupling, *triad_parts = halving_sum([coupling_part] + pack_mirror(triad_rows.reshape(cube)))
    triads = unpack_mirror(*triad_parts).reshape(extent, extent * extent)
    covariance = covariance / samples
    third_moment = third_moment / samples
    triads = triads / cell_count
    coupling = coupling / cell_count
    weights = pairs - covariance.reshape(extent * extent)[:, None]
    quadratic = jnp.dot(triads, weights, precision=FAST)
    new_coefficients = centered + TIME_STEP * (matmul(coupling, centered) + quadratic)
    weighted = fast_matmul(covariance.T, flattened)
    new_mean = mean_flat + TIME_STEP * (
        -mean_flat * mean_gradient + VISCOSITY * mean_smooth - jnp.sum(weighted * gradient, axis=0)
    )
    moment_flat = third_moment.reshape(extent, extent * extent)
    moment_term = fast_matmul(moment_flat, products)
    forcing = fast_matmul(covariance, linear) - moment_term
    half_power = inverse_root(covariance)
    weighting = matmul(half_power, half_power)
    projection = matmul(covariance, coupling.T) + matmul(moment_flat, triads.T)
    residual = forcing - fast_matmul(projection, flattened)
    stepped = flattened + TIME_STEP * fast_matmul(weighting, residual)
    gram_matrix = doubling_sum(matmul(stepped, stepped.T)) / cell_count
    factor = jnp.linalg.cholesky(gram_matrix)
    new_modes = lax.linalg.triangular_solve(factor, stepped, left_side=True, lower=True)
    return (
        new_modes.reshape(mode_fields.shape),
        new_mean.reshape(mean_field.shape),
        new_coefficients,
    )


def solution(mesh):
    placed = (P(None, "gy", "gx"), P("gy", "gx"), P(None, ("gx", "gy")))
    return jax.shard_map(
        per_device,
        mesh=mesh,
        in_specs=placed,
        out_specs=(P(None, "gy", "gx"), P("gy", "gx"), P(None, ("gx", "gy"))),
        check_vma=False,
    )
```

```python
import jax
import jax.numpy as jnp
import numpy as np
from jax import lax
from jax.sharding import PartitionSpec as P

NS_ITERS = 6


TIME_STEP = 0.02
VISCOSITY = 0.25
PRECISE = lax.Precision.HIGHEST
FAST = lax.Precision.HIGH


AXES = ("gx", "gy")


def device_count():
    return lax.axis_size("gx") * lax.axis_size("gy")


def linear_index():
    return lax.axis_index("gx") * lax.axis_size("gy") + lax.axis_index("gy")


def exchange_bits():
    count = device_count()
    bits = [1 << b for b in range(count.bit_length() - 1)]
    first = lax.axis_size("gy")
    return [first] + [bit for bit in bits if bit != first]


def swap(values, bit):
    count = device_count()
    return lax.ppermute(values, AXES, [(i, i ^ bit) for i in range(count)])


def doubling_sum(values):
    count = device_count()
    if count & (count - 1):
        return lax.psum(values, AXES)
    for bit in exchange_bits():
        values = values + swap(values, bit)
    return values


def halving_sum(parts):
    count = device_count()
    if count & (count - 1):
        return lax.psum(parts, AXES)
    shapes = [part.shape for part in parts]
    flat = jnp.concatenate([part.reshape(-1) for part in parts])
    total = flat.shape[0]
    unit = count * 128
    padded = -(-total // unit) * unit
    flat = jnp.pad(flat, (0, padded - total)).reshape(padded // 128, 128)
    me = linear_index()
    bits = exchange_bits()
    for bit in bits:
        half = flat.shape[0] // 2
        upper = (me // bit) % 2
        keep = lax.dynamic_slice_in_dim(flat, upper * half, half)
        send = lax.dynamic_slice_in_dim(flat, (1 - upper) * half, half)
        flat = keep + swap(send, bit)
    for bit in reversed(bits):
        upper = (me // bit) % 2
        other = swap(flat, bit)
        both = jnp.zeros((2 * flat.shape[0], 128), flat.dtype)
        both = lax.dynamic_update_slice_in_dim(both, flat, upper * flat.shape[0], 0)
        flat = lax.dynamic_update_slice_in_dim(both, other, (1 - upper) * flat.shape[0], 0)
    flat = flat.reshape(-1)[:total]
    out, start = [], 0
    for shape in shapes:
        size = int(np.prod(shape))
        out.append(flat[start:start + size].reshape(shape))
        start += size
    return out


def mirror_masks(half):
    row = lax.broadcasted_iota(jnp.int32, (half, half, 1), 0)
    col = lax.broadcasted_iota(jnp.int32, (half, half, 1), 1)
    return row, col


def pack_mirror(values):
    if values.shape[0] % 2:
        return [values]
    half = values.shape[0] // 2
    row, col = mirror_masks(half)
    upper = values[:half, half:]
    lower = values[half:, half:]
    merged = jnp.where(row >= col, values[:half, :half], lower)
    diagonal = jnp.sum(jnp.where(row == col, lower, 0.0), axis=1)
    return [upper, merged, diagonal]


def unpack_mirror(*parts):
    if len(parts) == 1:
        return parts[0]
    upper, merged, diagonal = parts
    row, col = mirror_masks(merged.shape[0])
    flipped = jnp.transpose(merged, (1, 0, 2))
    first = jnp.where(row >= col, merged, flipped)
    last = jnp.where(row < col, merged, jnp.where(row > col, flipped, diagonal[:, None, :]))
    top = jnp.concatenate([first, upper], axis=1)
    bottom = jnp.concatenate([jnp.transpose(upper, (1, 0, 2)), last], axis=1)
    return jnp.concatenate([top, bottom], axis=0)


def shift_pair(array, axis, dim):
    size, length = (lax.axis_size(axis), array.shape[dim])
    up = [(i, (i + 1) % size) for i in range(size)]
    down = [(j, i) for i, j in up]
    last = lax.slice_in_dim(array, length - 1, length, axis=dim)
    first = lax.slice_in_dim(array, 0, 1, axis=dim)
    return lax.ppermute(last, axis, up), lax.ppermute(first, axis, down)


def padded_cross(array):
    west, east = shift_pair(array, "gx", 2)
    south, north = shift_pair(array, "gy", 1)
    middle = jnp.concatenate([west, array, east], axis=2)
    corners = ((0, 0), (0, 0), (1, 1))
    return jnp.concatenate([jnp.pad(south, corners), middle, jnp.pad(north, corners)], axis=1)


def matmul(left, right):
    return jnp.dot(left, right, precision=PRECISE)


def fast_matmul(left, right):
    return jnp.dot(left, right, precision=FAST)


def pair_index(extent):
    flat_pairs = np.arange(extent * extent)
    leading = flat_pairs // extent
    trailing = flat_pairs % extent
    return (leading, trailing)


def pair_rows(values):
    extent = values.shape[0]
    return (values[:, None, :] * values[None, :, :]).reshape(extent * extent, values.shape[1])


def inverse_root(covariance):
    identity = jnp.eye(covariance.shape[0], dtype=jnp.float32)
    scaling = jnp.sqrt(jnp.sum(covariance * covariance) + 1e-06)
    current = covariance / scaling
    inverse = identity
    for iteration in range(NS_ITERS):
        middle = 0.5 * (3.0 * identity - matmul(inverse, current))
        current = matmul(current, middle)
        inverse = matmul(middle, inverse)
    return inverse / jnp.sqrt(scaling)


def per_device(mode_fields, mean_field, coefficients):
    extent = mode_fields.shape[0]
    devices = lax.axis_size("gx") * lax.axis_size("gy")
    local_cells = mode_fields.shape[1] * mode_fields.shape[2]
    cell_count = local_cells * devices
    samples = coefficients.shape[1] * devices
    stacked = jnp.concatenate([mean_field[None], mode_fields], axis=0)
    padded = padded_cross(stacked)
    middle = padded[:, 1:-1, 1:-1]
    western = padded[:, 1:-1, :-2]
    eastern = padded[:, 1:-1, 2:]
    southern = padded[:, :-2, 1:-1]
    northern = padded[:, 2:, 1:-1]
    upwinded = (2.0 * middle - western - southern).reshape(extent + 1, local_cells)
    smoothed = (western + eastern + southern + northern - 4.0 * middle).reshape(
        extent + 1, local_cells
    )
    mean_flat = mean_field.reshape(local_cells)
    mean_gradient = upwinded[0]
    mean_smooth = smoothed[0]
    gradient = upwinded[1:]
    flattened = mode_fields.reshape(extent, local_cells)
    linear = -mean_flat * gradient - flattened * mean_gradient + VISCOSITY * smoothed[1:]
    coupling_part = fast_matmul(flattened, linear.T)
    products = (flattened[:, None, :] * gradient[None, :, :]).reshape(extent * extent, local_cells)
    triad_rows = -fast_matmul(flattened, products.T)
    totals = doubling_sum(jnp.sum(coefficients, axis=1) + 0.0 * mean_gradient[0])
    sample_mean = totals / samples
    centered = coefficients - sample_mean[:, None]
    pairs = pair_rows(centered)
    cube = (extent, extent, extent)
    covariance, *third_parts = halving_sum(
        [matmul(centered, centered.T)] + pack_mirror(fast_matmul(pairs, centered.T).reshape(cube))
    )
    third_moment = unpack_mirror(*third_parts).reshape(extent * extent, extent)
    coupling, *triad_parts = halving_sum([coupling_part] + pack_mirror(triad_rows.reshape(cube)))
    triads = unpack_mirror(*triad_parts).reshape(extent, extent * extent)
    covariance = covariance / samples
    third_moment = third_moment / samples
    triads = triads / cell_count
    coupling = coupling / cell_count
    weights = pairs - covariance.reshape(extent * extent)[:, None]
    quadratic = jnp.dot(triads, weights, precision=FAST)
    new_coefficients = centered + TIME_STEP * (matmul(coupling, centered) + quadratic)
    weighted = fast_matmul(covariance.T, flattened)
    new_mean = mean_flat + TIME_STEP * (
        -mean_flat * mean_gradient + VISCOSITY * mean_smooth - jnp.sum(weighted * gradient, axis=0)
    )
    moment_flat = third_moment.reshape(extent, extent * extent)
    moment_term = fast_matmul(moment_flat, products)
    forcing = fast_matmul(covariance, linear) - moment_term
    half_power = inverse_root(covariance)
    weighting = matmul(half_power, half_power)
    projection = matmul(covariance, coupling.T) + matmul(moment_flat, triads.T)
    residual = forcing - fast_matmul(projection, flattened)
    stepped = flattened + TIME_STEP * fast_matmul(weighting, residual)
    gram_matrix = doubling_sum(matmul(stepped, stepped.T)) / cell_count
    factor = jnp.linalg.cholesky(gram_matrix)
    new_modes = lax.linalg.triangular_solve(factor, stepped, left_side=True, lower=True)
    return (
        new_modes.reshape(mode_fields.shape),
        new_mean.reshape(mean_field.shape),
        new_coefficients,
    )


def solution(mesh):
    placed = (P(None, "gy", "gx"), P("gy", "gx"), P(None, ("gx", "gy")))
    return jax.shard_map(
        per_device,
        mesh=mesh,
        in_specs=placed,
        out_specs=(P(None, "gy", "gx"), P("gy", "gx"), P(None, ("gx", "gy"))),
        check_vma=False,
    )
```

```python
import jax
import jax.numpy as jnp
import numpy as np
from jax import lax
from jax.sharding import PartitionSpec as P

NS_ITERS = 6


TIME_STEP = 0.02
VISCOSITY = 0.25
PRECISE = lax.Precision.HIGHEST
FAST = lax.Precision.HIGH


AXES = ("gx", "gy")


def device_count():
    return lax.axis_size("gx") * lax.axis_size("gy")


def linear_index():
    return lax.axis_index("gx") * lax.axis_size("gy") + lax.axis_index("gy")


def exchange_bits():
    count = device_count()
    bits = [1 << b for b in range(count.bit_length() - 1)]
    first = lax.axis_size("gy")
    return [first] + [bit for bit in bits if bit != first]


def swap(values, bit):
    count = device_count()
    return lax.ppermute(values, AXES, [(i, i ^ bit) for i in range(count)])


def doubling_sum(values):
    count = device_count()
    if count & (count - 1):
        return lax.psum(values, AXES)
    for bit in exchange_bits():
        values = values + swap(values, bit)
    return values


def halving_sum(parts):
    count = device_count()
    if count & (count - 1):
        return lax.psum(parts, AXES)
    shapes = [part.shape for part in parts]
    flat = jnp.concatenate([part.reshape(-1) for part in parts])
    total = flat.shape[0]
    unit = count * 128
    padded = -(-total // unit) * unit
    flat = jnp.pad(flat, (0, padded - total)).reshape(padded // 128, 128)
    me = linear_index()
    bits = exchange_bits()
    for bit in bits:
        half = flat.shape[0] // 2
        upper = (me // bit) % 2
        keep = lax.dynamic_slice_in_dim(flat, upper * half, half)
        send = lax.dynamic_slice_in_dim(flat, (1 - upper) * half, half)
        flat = keep + swap(send, bit)
    for bit in reversed(bits):
        upper = (me // bit) % 2
        other = swap(flat, bit)
        both = jnp.zeros((2 * flat.shape[0], 128), flat.dtype)
        both = lax.dynamic_update_slice_in_dim(both, flat, upper * flat.shape[0], 0)
        flat = lax.dynamic_update_slice_in_dim(both, other, (1 - upper) * flat.shape[0], 0)
    flat = flat.reshape(-1)[:total]
    out, start = [], 0
    for shape in shapes:
        size = int(np.prod(shape))
        out.append(flat[start:start + size].reshape(shape))
        start += size
    return out


def mirror_masks(half):
    row = lax.broadcasted_iota(jnp.int32, (half, half, 1), 0)
    col = lax.broadcasted_iota(jnp.int32, (half, half, 1), 1)
    return row, col


def pack_mirror(values):
    if values.shape[0] % 2:
        return [values]
    half = values.shape[0] // 2
    row, col = mirror_masks(half)
    upper = values[:half, half:]
    lower = values[half:, half:]
    merged = jnp.where(row >= col, values[:half, :half], lower)
    diagonal = jnp.sum(jnp.where(row == col, lower, 0.0), axis=1)
    return [upper, merged, diagonal]


def unpack_mirror(*parts):
    if len(parts) == 1:
        return parts[0]
    upper, merged, diagonal = parts
    row, col = mirror_masks(merged.shape[0])
    flipped = jnp.transpose(merged, (1, 0, 2))
    first = jnp.where(row >= col, merged, flipped)
    last = jnp.where(row < col, merged, jnp.where(row > col, flipped, diagonal[:, None, :]))
    top = jnp.concatenate([first, upper], axis=1)
    bottom = jnp.concatenate([jnp.transpose(upper, (1, 0, 2)), last], axis=1)
    return jnp.concatenate([top, bottom], axis=0)


def shift_pair(array, axis, dim):
    size, length = (lax.axis_size(axis), array.shape[dim])
    up = [(i, (i + 1) % size) for i in range(size)]
    down = [(j, i) for i, j in up]
    last = lax.slice_in_dim(array, length - 1, length, axis=dim)
    first = lax.slice_in_dim(array, 0, 1, axis=dim)
    return lax.ppermute(last, axis, up), lax.ppermute(first, axis, down)


def padded_cross(array):
    west, east = shift_pair(array, "gx", 2)
    south, north = shift_pair(array, "gy", 1)
    middle = jnp.concatenate([west, array, east], axis=2)
    corners = ((0, 0), (0, 0), (1, 1))
    return jnp.concatenate([jnp.pad(south, corners), middle, jnp.pad(north, corners)], axis=1)


def matmul(left, right):
    return jnp.dot(left, right, precision=PRECISE)


def fast_matmul(left, right):
    return jnp.dot(left, right, precision=FAST)


def pair_index(extent):
    flat_pairs = np.arange(extent * extent)
    leading = flat_pairs // extent
    trailing = flat_pairs % extent
    return (leading, trailing)


def pair_rows(values):
    extent = values.shape[0]
    return (values[:, None, :] * values[None, :, :]).reshape(extent * extent, values.shape[1])


def inverse_root(covariance):
    identity = jnp.eye(covariance.shape[0], dtype=jnp.float32)
    scaling = jnp.sqrt(jnp.sum(covariance * covariance) + 1e-06)
    current = covariance / scaling
    inverse = identity
    for iteration in range(NS_ITERS):
        middle = 0.5 * (3.0 * identity - matmul(inverse, current))
        current = matmul(current, middle)
        inverse = matmul(middle, inverse)
    return inverse / jnp.sqrt(scaling)


def per_device(mode_fields, mean_field, coefficients):
    extent = mode_fields.shape[0]
    devices = lax.axis_size("gx") * lax.axis_size("gy")
    local_cells = mode_fields.shape[1] * mode_fields.shape[2]
    cell_count = local_cells * devices
    samples = coefficients.shape[1] * devices
    stacked = jnp.concatenate([mean_field[None], mode_fields], axis=0)
    padded = padded_cross(stacked)
    middle = padded[:, 1:-1, 1:-1]
    western = padded[:, 1:-1, :-2]
    eastern = padded[:, 1:-1, 2:]
    southern = padded[:, :-2, 1:-1]
    northern = padded[:, 2:, 1:-1]
    upwinded = (2.0 * middle - western - southern).reshape(extent + 1, local_cells)
    smoothed = (western + eastern + southern + northern - 4.0 * middle).reshape(
        extent + 1, local_cells
    )
    mean_flat = mean_field.reshape(local_cells)
    mean_gradient = upwinded[0]
    mean_smooth = smoothed[0]
    gradient = upwinded[1:]
    flattened = mode_fields.reshape(extent, local_cells)
    linear = -mean_flat * gradient - flattened * mean_gradient + VISCOSITY * smoothed[1:]
    coupling_part = fast_matmul(flattened, linear.T)
    products = (flattened[:, None, :] * gradient[None, :, :]).reshape(extent * extent, local_cells)
    triad_rows = -fast_matmul(flattened, products.T)
    totals = doubling_sum(jnp.sum(coefficients, axis=1))
    sample_mean = totals / samples
    centered = coefficients - sample_mean[:, None]
    pairs = pair_rows(centered)
    cube = (extent, extent, extent)
    covariance, *third_parts = halving_sum(
        [matmul(centered, centered.T)] + pack_mirror(fast_matmul(pairs, centered.T).reshape(cube))
    )
    third_moment = unpack_mirror(*third_parts).reshape(extent * extent, extent)
    coupling, *triad_parts = halving_sum([coupling_part] + pack_mirror(triad_rows.reshape(cube)))
    triads = unpack_mirror(*triad_parts).reshape(extent, extent * extent)
    covariance = covariance / samples
    third_moment = third_moment / samples
    triads = triads / cell_count
    coupling = coupling / cell_count
    weights = pairs - covariance.reshape(extent * extent)[:, None]
    quadratic = jnp.dot(triads, weights, precision=FAST)
    new_coefficients = centered + TIME_STEP * (matmul(coupling, centered) + quadratic)
    weighted = fast_matmul(covariance.T, flattened)
    new_mean = mean_flat + TIME_STEP * (
        -mean_flat * mean_gradient + VISCOSITY * mean_smooth - jnp.sum(weighted * gradient, axis=0)
    )
    moment_flat = third_moment.reshape(extent, extent * extent)
    moment_term = fast_matmul(moment_flat, products)
    forcing = fast_matmul(covariance, linear) - moment_term
    half_power = inverse_root(covariance)
    weighting = matmul(half_power, half_power)
    projection = matmul(covariance, coupling.T) + fast_matmul(moment_flat, triads.T)
    residual = forcing - fast_matmul(projection, flattened)
    stepped = flattened + TIME_STEP * fast_matmul(weighting, residual)
    gram_matrix = doubling_sum(matmul(stepped, stepped.T)) / cell_count
    factor = jnp.linalg.cholesky(gram_matrix)
    new_modes = lax.linalg.triangular_solve(factor, stepped, left_side=True, lower=True)
    return (
        new_modes.reshape(mode_fields.shape),
        new_mean.reshape(mean_field.shape),
        new_coefficients,
    )


def solution(mesh):
    placed = (P(None, "gy", "gx"), P("gy", "gx"), P(None, ("gx", "gy")))
    return jax.shard_map(
        per_device,
        mesh=mesh,
        in_specs=placed,
        out_specs=(P(None, "gy", "gx"), P("gy", "gx"), P(None, ("gx", "gy"))),
        check_vma=False,
    )
```

```python
import jax
import jax.numpy as jnp
import numpy as np
from jax import lax
from jax.sharding import PartitionSpec as P

NS_ITERS = 6


TIME_STEP = 0.02
VISCOSITY = 0.25
PRECISE = lax.Precision.HIGHEST
FAST = lax.Precision.HIGH


AXES = ("gx", "gy")


def device_count():
    return lax.axis_size("gx") * lax.axis_size("gy")


def linear_index():
    return lax.axis_index("gx") * lax.axis_size("gy") + lax.axis_index("gy")


def exchange_bits():
    count = device_count()
    bits = [1 << b for b in range(count.bit_length() - 1)]
    first = lax.axis_size("gy")
    return [first] + [bit for bit in bits if bit != first]


def swap(values, bit):
    count = device_count()
    return lax.ppermute(values, AXES, [(i, i ^ bit) for i in range(count)])


def doubling_sum(values):
    count = device_count()
    if count & (count - 1):
        return lax.psum(values, AXES)
    for bit in exchange_bits():
        values = values + swap(values, bit)
    return values


def halving_sum(parts):
    count = device_count()
    if count & (count - 1):
        return lax.psum(parts, AXES)
    shapes = [part.shape for part in parts]
    flat = jnp.concatenate([part.reshape(-1) for part in parts])
    total = flat.shape[0]
    unit = count * 128
    padded = -(-total // unit) * unit
    flat = jnp.pad(flat, (0, padded - total)).reshape(padded // 128, 128)
    me = linear_index()
    bits = exchange_bits()
    for bit in bits:
        half = flat.shape[0] // 2
        upper = (me // bit) % 2
        keep = lax.dynamic_slice_in_dim(flat, upper * half, half)
        send = lax.dynamic_slice_in_dim(flat, (1 - upper) * half, half)
        flat = keep + swap(send, bit)
    for bit in reversed(bits):
        upper = (me // bit) % 2
        other = swap(flat, bit)
        both = jnp.zeros((2 * flat.shape[0], 128), flat.dtype)
        both = lax.dynamic_update_slice_in_dim(both, flat, upper * flat.shape[0], 0)
        flat = lax.dynamic_update_slice_in_dim(both, other, (1 - upper) * flat.shape[0], 0)
    flat = flat.reshape(-1)[:total]
    out, start = [], 0
    for shape in shapes:
        size = int(np.prod(shape))
        out.append(flat[start:start + size].reshape(shape))
        start += size
    return out


def mirror_masks(half):
    row = lax.broadcasted_iota(jnp.int32, (half, half, 1), 0)
    col = lax.broadcasted_iota(jnp.int32, (half, half, 1), 1)
    return row, col


def pack_mirror(values):
    if values.shape[0] % 2:
        return [values]
    half = values.shape[0] // 2
    row, col = mirror_masks(half)
    upper = values[:half, half:]
    lower = values[half:, half:]
    merged = jnp.where(row >= col, values[:half, :half], lower)
    diagonal = lower.reshape((half * half,) + lower.shape[2:])[:: half + 1]
    return [upper, merged, diagonal]


def unpack_mirror(*parts):
    if len(parts) == 1:
        return parts[0]
    upper, merged, diagonal = parts
    row, col = mirror_masks(merged.shape[0])
    flipped = jnp.transpose(merged, (1, 0, 2))
    first = jnp.where(row >= col, merged, flipped)
    last = jnp.where(row < col, merged, jnp.where(row > col, flipped, diagonal[:, None, :]))
    top = jnp.concatenate([first, upper], axis=1)
    bottom = jnp.concatenate([jnp.transpose(upper, (1, 0, 2)), last], axis=1)
    return jnp.concatenate([top, bottom], axis=0)


def shift_pair(array, axis, dim):
    size, length = (lax.axis_size(axis), array.shape[dim])
    up = [(i, (i + 1) % size) for i in range(size)]
    down = [(j, i) for i, j in up]
    last = lax.slice_in_dim(array, length - 1, length, axis=dim)
    first = lax.slice_in_dim(array, 0, 1, axis=dim)
    return lax.ppermute(last, axis, up), lax.ppermute(first, axis, down)


def padded_cross(array):
    west, east = shift_pair(array, "gx", 2)
    south, north = shift_pair(array, "gy", 1)
    middle = jnp.concatenate([west, array, east], axis=2)
    corners = ((0, 0), (0, 0), (1, 1))
    return jnp.concatenate([jnp.pad(south, corners), middle, jnp.pad(north, corners)], axis=1)


def matmul(left, right):
    return jnp.dot(left, right, precision=PRECISE)


def fast_matmul(left, right):
    return jnp.dot(left, right, precision=FAST)


def pair_index(extent):
    flat_pairs = np.arange(extent * extent)
    leading = flat_pairs // extent
    trailing = flat_pairs % extent
    return (leading, trailing)


def pair_rows(values):
    extent = values.shape[0]
    return (values[:, None, :] * values[None, :, :]).reshape(extent * extent, values.shape[1])


def inverse_root(covariance):
    identity = jnp.eye(covariance.shape[0], dtype=jnp.float32)
    scaling = jnp.sqrt(jnp.sum(covariance * covariance) + 1e-06)
    current = covariance / scaling
    inverse = identity
    for iteration in range(NS_ITERS):
        middle = 0.5 * (3.0 * identity - matmul(inverse, current))
        current = matmul(current, middle)
        inverse = matmul(middle, inverse)
    return inverse / jnp.sqrt(scaling)


def per_device(mode_fields, mean_field, coefficients):
    extent = mode_fields.shape[0]
    devices = lax.axis_size("gx") * lax.axis_size("gy")
    local_cells = mode_fields.shape[1] * mode_fields.shape[2]
    cell_count = local_cells * devices
    samples = coefficients.shape[1] * devices
    stacked = jnp.concatenate([mean_field[None], mode_fields], axis=0)
    padded = padded_cross(stacked)
    middle = padded[:, 1:-1, 1:-1]
    western = padded[:, 1:-1, :-2]
    eastern = padded[:, 1:-1, 2:]
    southern = padded[:, :-2, 1:-1]
    northern = padded[:, 2:, 1:-1]
    upwinded = (2.0 * middle - western - southern).reshape(extent + 1, local_cells)
    smoothed = (western + eastern + southern + northern - 4.0 * middle).reshape(
        extent + 1, local_cells
    )
    mean_flat = mean_field.reshape(local_cells)
    mean_gradient = upwinded[0]
    mean_smooth = smoothed[0]
    gradient = upwinded[1:]
    flattened = mode_fields.reshape(extent, local_cells)
    linear = -mean_flat * gradient - flattened * mean_gradient + VISCOSITY * smoothed[1:]
    coupling_part = fast_matmul(flattened, linear.T)
    products = (flattened[:, None, :] * gradient[None, :, :]).reshape(extent * extent, local_cells)
    triad_rows = -fast_matmul(flattened, products.T)
    totals = doubling_sum(jnp.sum(coefficients, axis=1))
    sample_mean = totals / samples
    centered = coefficients - sample_mean[:, None]
    pairs = pair_rows(centered)
    cube = (extent, extent, extent)
    covariance, *third_parts = halving_sum(
        [matmul(centered, centered.T)] + pack_mirror(fast_matmul(pairs, centered.T).reshape(cube))
    )
    third_moment = unpack_mirror(*third_parts).reshape(extent * extent, extent)
    coupling, *triad_parts = halving_sum([coupling_part] + pack_mirror(triad_rows.reshape(cube)))
    triads = unpack_mirror(*triad_parts).reshape(extent, extent * extent)
    covariance = covariance / samples
    third_moment = third_moment / samples
    triads = triads / cell_count
    coupling = coupling / cell_count
    weights = pairs - covariance.reshape(extent * extent)[:, None]
    quadratic = jnp.dot(triads, weights, precision=FAST)
    new_coefficients = centered + TIME_STEP * (matmul(coupling, centered) + quadratic)
    weighted = fast_matmul(covariance.T, flattened)
    new_mean = mean_flat + TIME_STEP * (
        -mean_flat * mean_gradient + VISCOSITY * mean_smooth - jnp.sum(weighted * gradient, axis=0)
    )
    moment_flat = third_moment.reshape(extent, extent * extent)
    moment_term = fast_matmul(moment_flat, products)
    forcing = fast_matmul(covariance, linear) - moment_term
    half_power = inverse_root(covariance)
    weighting = matmul(half_power, half_power)
    projection = matmul(covariance, coupling.T) + matmul(moment_flat, triads.T)
    residual = forcing - fast_matmul(projection, flattened)
    stepped = flattened + TIME_STEP * fast_matmul(weighting, residual)
    gram_matrix = doubling_sum(matmul(stepped, stepped.T)) / cell_count
    factor = jnp.linalg.cholesky(gram_matrix)
    new_modes = lax.linalg.triangular_solve(factor, stepped, left_side=True, lower=True)
    return (
        new_modes.reshape(mode_fields.shape),
        new_mean.reshape(mean_field.shape),
        new_coefficients,
    )


def solution(mesh):
    placed = (P(None, "gy", "gx"), P("gy", "gx"), P(None, ("gx", "gy")))
    return jax.shard_map(
        per_device,
        mesh=mesh,
        in_specs=placed,
        out_specs=(P(None, "gy", "gx"), P("gy", "gx"), P(None, ("gx", "gy"))),
        check_vma=False,
    )
```

```python
import jax
import jax.numpy as jnp
import numpy as np
from jax import lax
from jax.sharding import PartitionSpec as P

NS_ITERS = 6


TIME_STEP = 0.02
VISCOSITY = 0.25
PRECISE = lax.Precision.HIGHEST
FAST = lax.Precision.HIGH


AXES = ("gx", "gy")


def device_count():
    return lax.axis_size("gx") * lax.axis_size("gy")


def linear_index():
    return lax.axis_index("gx") * lax.axis_size("gy") + lax.axis_index("gy")


def exchange_bits():
    count = device_count()
    bits = [1 << b for b in range(count.bit_length() - 1)]
    first = lax.axis_size("gy")
    return [first] + [bit for bit in bits if bit != first]


def swap(values, bit):
    count = device_count()
    return lax.ppermute(values, AXES, [(i, i ^ bit) for i in range(count)])


def doubling_sum(values):
    count = device_count()
    if count & (count - 1):
        return lax.psum(values, AXES)
    for bit in exchange_bits():
        values = values + swap(values, bit)
    return values


def halving_sum(parts):
    count = device_count()
    if count & (count - 1):
        return lax.psum(parts, AXES)
    shapes = [part.shape for part in parts]
    flat = jnp.concatenate([part.reshape(-1) for part in parts])
    total = flat.shape[0]
    unit = count * 128
    padded = -(-total // unit) * unit
    flat = jnp.pad(flat, (0, padded - total)).reshape(padded // 128, 128)
    me = linear_index()
    bits = exchange_bits()
    for bit in bits:
        half = flat.shape[0] // 2
        upper = (me // bit) % 2
        keep = lax.dynamic_slice_in_dim(flat, upper * half, half)
        send = lax.dynamic_slice_in_dim(flat, (1 - upper) * half, half)
        flat = keep + swap(send, bit)
    for bit in reversed(bits):
        upper = (me // bit) % 2
        other = swap(flat, bit)
        both = jnp.zeros((2 * flat.shape[0], 128), flat.dtype)
        both = lax.dynamic_update_slice_in_dim(both, flat, upper * flat.shape[0], 0)
        flat = lax.dynamic_update_slice_in_dim(both, other, (1 - upper) * flat.shape[0], 0)
    flat = flat.reshape(-1)[:total]
    out, start = [], 0
    for shape in shapes:
        size = int(np.prod(shape))
        out.append(flat[start:start + size].reshape(shape))
        start += size
    return out


def mirror_masks(half):
    row = lax.broadcasted_iota(jnp.int32, (half, half, 1), 0)
    col = lax.broadcasted_iota(jnp.int32, (half, half, 1), 1)
    return row, col


def pack_mirror(values):
    if values.shape[0] % 2:
        return [values]
    half = values.shape[0] // 2
    row, col = mirror_masks(half)
    upper = values[:half, half:]
    lower = values[half:, half:]
    merged = jnp.where(row >= col, values[:half, :half], lower)
    diagonal = lower.reshape((half * half,) + lower.shape[2:])[:: half + 1]
    return [upper, merged, diagonal]


def unpack_mirror(*parts):
    if len(parts) == 1:
        return parts[0]
    upper, merged, diagonal = parts
    row, col = mirror_masks(merged.shape[0])
    flipped = jnp.transpose(merged, (1, 0, 2))
    first = jnp.where(row >= col, merged, flipped)
    last = jnp.where(row < col, merged, jnp.where(row > col, flipped, diagonal[:, None, :]))
    top = jnp.concatenate([first, upper], axis=1)
    bottom = jnp.concatenate([jnp.transpose(upper, (1, 0, 2)), last], axis=1)
    return jnp.concatenate([top, bottom], axis=0)


def shift_pair(array, axis, dim):
    size, length = (lax.axis_size(axis), array.shape[dim])
    up = [(i, (i + 1) % size) for i in range(size)]
    down = [(j, i) for i, j in up]
    last = lax.slice_in_dim(array, length - 1, length, axis=dim)
    first = lax.slice_in_dim(array, 0, 1, axis=dim)
    return lax.ppermute(last, axis, up), lax.ppermute(first, axis, down)


def padded_cross(array):
    west, east = shift_pair(array, "gx", 2)
    south, north = shift_pair(array, "gy", 1)
    middle = jnp.concatenate([west, array, east], axis=2)
    corners = ((0, 0), (0, 0), (1, 1))
    return jnp.concatenate([jnp.pad(south, corners), middle, jnp.pad(north, corners)], axis=1)


def matmul(left, right):
    return jnp.dot(left, right, precision=PRECISE)


def fast_matmul(left, right):
    return jnp.dot(left, right, precision=FAST)


def pair_index(extent):
    flat_pairs = np.arange(extent * extent)
    leading = flat_pairs // extent
    trailing = flat_pairs % extent
    return (leading, trailing)


def pair_rows(values):
    extent = values.shape[0]
    return (values[:, None, :] * values[None, :, :]).reshape(extent * extent, values.shape[1])


def inverse_root(covariance):
    identity = jnp.eye(covariance.shape[0], dtype=jnp.float32)
    scaling = jnp.sqrt(jnp.sum(covariance * covariance) + 1e-06)
    current = covariance / scaling
    inverse = identity
    for iteration in range(NS_ITERS):
        middle = 0.5 * (3.0 * identity - matmul(inverse, current))
        current = matmul(current, middle)
        inverse = matmul(middle, inverse)
    return inverse / jnp.sqrt(scaling)


def per_device(mode_fields, mean_field, coefficients):
    extent = mode_fields.shape[0]
    devices = lax.axis_size("gx") * lax.axis_size("gy")
    local_cells = mode_fields.shape[1] * mode_fields.shape[2]
    cell_count = local_cells * devices
    samples = coefficients.shape[1] * devices
    stacked = jnp.concatenate([mean_field[None], mode_fields], axis=0)
    padded = padded_cross(stacked)
    middle = padded[:, 1:-1, 1:-1]
    western = padded[:, 1:-1, :-2]
    eastern = padded[:, 1:-1, 2:]
    southern = padded[:, :-2, 1:-1]
    northern = padded[:, 2:, 1:-1]
    upwinded = (2.0 * middle - western - southern).reshape(extent + 1, local_cells)
    smoothed = (western + eastern + southern + northern - 4.0 * middle).reshape(
        extent + 1, local_cells
    )
    mean_flat = mean_field.reshape(local_cells)
    mean_gradient = upwinded[0]
    mean_smooth = smoothed[0]
    gradient = upwinded[1:]
    flattened = mode_fields.reshape(extent, local_cells)
    linear = -mean_flat * gradient - flattened * mean_gradient + VISCOSITY * smoothed[1:]
    coupling_part = fast_matmul(flattened, linear.T)
    products = (flattened[:, None, :] * gradient[None, :, :]).reshape(extent * extent, local_cells)
    triad_rows = -lax.dot_general(
        flattened, products.reshape(extent, extent, local_cells), (((1,), (2,)), ((), ())), precision=FAST
    )
    totals = doubling_sum(jnp.sum(coefficients, axis=1))
    sample_mean = totals / samples
    centered = coefficients - sample_mean[:, None]
    pairs = pair_rows(centered)
    cube = (extent, extent, extent)
    covariance, *third_parts = halving_sum(
        [matmul(centered, centered.T)] + pack_mirror(fast_matmul(pairs, centered.T).reshape(cube))
    )
    third_moment = unpack_mirror(*third_parts).reshape(extent * extent, extent)
    coupling, *triad_parts = halving_sum([coupling_part] + pack_mirror(triad_rows.reshape(cube)))
    triads = unpack_mirror(*triad_parts).reshape(extent, extent * extent)
    covariance = covariance / samples
    third_moment = third_moment / samples
    triads = triads / cell_count
    coupling = coupling / cell_count
    weights = pairs - covariance.reshape(extent * extent)[:, None]
    quadratic = jnp.dot(triads, weights, precision=FAST)
    new_coefficients = centered + TIME_STEP * (matmul(coupling, centered) + quadratic)
    weighted = fast_matmul(covariance.T, flattened)
    new_mean = mean_flat + TIME_STEP * (
        -mean_flat * mean_gradient + VISCOSITY * mean_smooth - jnp.sum(weighted * gradient, axis=0)
    )
    moment_flat = third_moment.reshape(extent, extent * extent)
    moment_term = fast_matmul(moment_flat, products)
    forcing = fast_matmul(covariance, linear) - moment_term
    half_power = inverse_root(covariance)
    weighting = matmul(half_power, half_power)
    projection = matmul(covariance, coupling.T) + matmul(moment_flat, triads.T)
    residual = forcing - fast_matmul(projection, flattened)
    stepped = flattened + TIME_STEP * fast_matmul(weighting, residual)
    gram_matrix = doubling_sum(matmul(stepped, stepped.T)) / cell_count
    factor = jnp.linalg.cholesky(gram_matrix)
    new_modes = lax.linalg.triangular_solve(factor, stepped, left_side=True, lower=True)
    return (
        new_modes.reshape(mode_fields.shape),
        new_mean.reshape(mean_field.shape),
        new_coefficients,
    )


def solution(mesh):
    placed = (P(None, "gy", "gx"), P("gy", "gx"), P(None, ("gx", "gy")))
    return jax.shard_map(
        per_device,
        mesh=mesh,
        in_specs=placed,
        out_specs=(P(None, "gy", "gx"), P("gy", "gx"), P(None, ("gx", "gy"))),
        check_vma=False,
    )
```
